256 devices in a mesh: head: 8 (over y, z_lo), blk: 32 (over z_hi, x, core).
Axes of the slice: x: 4, y: 4, z: 8 (z_hi: 4, z_lo: 2; z = z_hi * 2 + z_lo), core: 2. Of those that a mesh axis runs over, the one named last changes fastest.
Arguments:
- queries: bfloat16 [32768, 6144], P(('blk', 'head')), may hold values from -4.5 to 4.5
- key_states: bfloat16 [32768, 6144], P(('blk', 'head')), may hold values from -4.5 to 4.5
- value_states: bfloat16 [32768, 6144], P(('blk', 'head')), may hold values from -6 to 6
- block_lists: int32 [256, 8], P('blk'), may hold values from 0 to 255, as said below
- block_counts: int32 [256], P('blk'), may hold values from 1 to 8
- tile_order: int32 [256], replicated, may hold values from 0 to 255, each once
Outputs:
- attended: bfloat16 [32768, 6144], P(('blk', 'head'))
The draws below stay inside these ranges and needn't reach their ends.
Inputs may be any that keep to these rules, and one draw needn't show every extreme that they name: `block_lists`: entry 0 of row t is t itself; the entries of a row are distinct, and each names a tile whose shard of 8 tiles lies at most 3 shards from the shard of t, counted cyclically over the clip.
All inputs are finite; a program needn't handle non-finite values.
Results may differ from the reference program's by a relative error of at most 0.0095.
Values may be sent and summed in bfloat16 or wider, within the bound.
No kernel may reach another device: no remote copies, remote signals or barrier semaphores. Data moves between devices by JAX's collectives and lax.ppermute only.
A program may use at most 128 MiB of HBM per device.

```python
import jax
import jax.numpy as jnp
from jax import lax

H = 48
DH = 128
TILE = 128
REACH = 3
SLOTS = 8
TPS = 8
SEQ = 32768
NTILES = 256


def make_states(key, which):
    rows = SEQ
    width = H * DH
    own_key = jax.random.fold_in(key, 11 + which)
    base = jnp.clip(jax.random.normal(own_key, (rows, width), jnp.float32), -4.5, 4.5)
    return base.astype(jnp.bfloat16)


def draw_queries(key, part):
    return make_states(key, 0)


def draw_key_states(key, part):
    return make_states(key, 1)


def draw_block_lists(key, part):
    window_tiles = (2 * REACH + 1) * TPS
    shard_total = NTILES // TPS
    tile_index = jnp.arange(NTILES, dtype=jnp.int32)
    row_keys = jax.random.split(jax.random.fold_in(key, 31), NTILES)
    picks = jax.vmap(lambda row_key: jax.random.permutation(row_key, window_tiles - 1))(row_keys)[:, :SLOTS - 1]
    picks = picks.astype(jnp.int32)
    self_place = REACH * TPS + tile_index % TPS
    window_place = picks + (picks >= self_place[:, None]).astype(jnp.int32)
    offset = window_place // TPS - REACH
    local_tile = window_place % TPS
    shard = ((tile_index // TPS)[:, None] + offset) % shard_total
    listed = shard * TPS + local_tile
    return jnp.concatenate([tile_index[:, None], listed], axis=1).astype(jnp.int32)


def draw_block_counts(key, part):
    counts = jax.random.randint(jax.random.fold_in(key, 53), (NTILES,), 1, SLOTS + 1).astype(jnp.int32)
    counts = counts.at[0].set(SLOTS)
    counts = counts.at[1].set(1)
    return counts


def block_scale(stream_key, dims, cuts, low, high):
    gain, own = 1.0, jax.random.fold_in(stream_key, 6)
    for axis_at, shards_of in cuts:
        heights = jnp.exp(jax.random.uniform(jax.random.fold_in(own, axis_at), (shards_of,), jnp.float32, low / len(cuts), high / len(cuts)))
        gain = gain * jnp.repeat(heights, dims[axis_at] // shards_of).reshape([-1 if axis == axis_at else 1 for axis in range(len(dims))])
    return gain


def centred(stream_key, dims, scale, bound, cuts=(), kind=jnp.bfloat16):
    loudness = block_scale(stream_key, dims, cuts, -0.22, 0.18) if cuts else 1.0
    array = jax.random.normal(stream_key, dims, jnp.float32) * scale * loudness
    return jnp.minimum(jnp.maximum(array, -bound), bound).astype(kind)


def setup_inputs(seed: int = 0) -> dict:
    key_list = jax.random.split(jax.random.key(seed), 7)
    queries = draw_queries(jax.random.fold_in(key_list[6], 71), 0)
    key_states = draw_key_states(jax.random.fold_in(key_list[6], 71), 0)
    value_states = centred(key_list[2], (SEQ, H * DH), 1.0, 6.0, ((0, 256),))
    block_lists = draw_block_lists(jax.random.fold_in(key_list[6], 71), 0)
    block_counts = draw_block_counts(jax.random.fold_in(key_list[6], 71), 0)
    tile_order = jax.random.permutation(key_list[5], NTILES).astype(jnp.int32)
    return {"queries": queries, "key_states": key_states, "value_states": value_states, "block_lists": block_lists, "block_counts": block_counts, "tile_order": tile_order}


def reference(queries, key_states, value_states, block_lists, block_counts, tile_order):
    q_all = queries.reshape(NTILES, TILE, H, DH)
    k_all = key_states.reshape(NTILES, TILE, H, DH)
    v_all = value_states.reshape(NTILES, TILE, H, DH)
    slopes = 8.0 * jnp.power(2.0, -8.0 * jnp.arange(H).astype(jnp.float32) / H)
    scale = DH ** -0.5

    def one_tile(tile_index):
        listed = block_lists[tile_index]
        q_tile = q_all[tile_index].astype(jnp.float32)
        k_sel = k_all[listed].astype(jnp.float32)
        v_sel = v_all[listed].astype(jnp.float32)
        scores = jnp.einsum("ihd,cjhd->hicj", q_tile, k_sel) * scale
        distance = jnp.abs(tile_order[tile_index] - tile_order[listed]).astype(jnp.float32) / NTILES
        scores = scores - slopes[:, None, None, None] * distance[None, None, :, None]
        valid = jnp.arange(SLOTS, dtype=jnp.int32) < block_counts[tile_index]
        scores = jnp.where(valid[None, None, :, None], scores, -1e30).reshape(H, TILE, SLOTS * TILE)
        top = jnp.max(scores, axis=-1)
        weights = jnp.exp(scores - top[..., None]).astype(jnp.bfloat16)
        total = jnp.sum(weights.astype(jnp.float32), axis=-1)
        mixed = jnp.einsum("hik,khd->ihd", weights.astype(jnp.float32), v_sel.reshape(SLOTS * TILE, H, DH))
        return (mixed / total.T[:, :, None]).astype(jnp.bfloat16)

    result = lax.map(one_tile, jnp.arange(NTILES, dtype=jnp.int32))
    return result.reshape(SEQ, H * DH)
```

```python
import jax
import jax.numpy as jnp
from jax import lax
from jax.experimental import pallas as pl
from jax.experimental.pallas import tpu as pltpu
from jax.sharding import PartitionSpec as P

H = 48
DH = 128
TILE = 128
REACH = 3
SLOTS = 8

PIECE_OF_OFFSET = ((4, 1, 5, 0, 3, 2, 6), (5, 1, 3, 0, 6, 2, 4))


def permute(block, axis, route):
    return lax.ppermute(block, axis, route)


def shift_pairs(n, distance):
    return [(i, (i + distance) % n) for i in range(n)]


def attention_kernel(sw_ref, cnt_ref, bias_ref, q_ref, *refs, heads_local, scale):
    k_refs = refs[:SLOTS]
    v_refs = refs[SLOTS:2 * SLOTS]
    o_ref = refs[2 * SLOTS]
    i = pl.program_id(0)
    count = cnt_ref[i]
    for h in range(heads_local):
        cols = slice(h * DH, (h + 1) * DH)
        q = q_ref[:, cols]
        scores = []
        for c in range(SLOTS):
            k = k_refs[c][:, cols]
            s = lax.dot_general(q, k, (((1,), (1,)), ((), ())), preferred_element_type=jnp.float32)
            s = s * scale
            s = s - bias_ref[(i * SLOTS + c) * heads_local + h]
            s = jnp.where(c < count, s, -1e30)
            scores.append(s)
        top = scores[0].max(axis=1, keepdims=True)
        for c in range(1, SLOTS):
            top = jnp.maximum(top, scores[c].max(axis=1, keepdims=True))
        total = jnp.zeros((TILE, 1), jnp.float32)
        acc = jnp.zeros((TILE, DH), jnp.float32)
        for c in range(SLOTS):
            w = jnp.exp(scores[c] - top).astype(jnp.bfloat16)
            total = total + w.astype(jnp.float32).sum(axis=1, keepdims=True)
            acc = acc + jnp.dot(w, v_refs[c][:, cols], preferred_element_type=jnp.float32)
        o_ref[:, cols] = (acc / total).astype(o_ref.dtype)


def body(queries, key_states, value_states, block_lists, block_counts, tile_order):
    cycle_size = lax.axis_size("blk")
    group_size = lax.axis_size("head")
    heads_local = H // group_size
    k_heads, v_heads = (
        lax.all_to_all(key_states, "head", split_axis=1, concat_axis=0, tiled=True),
        lax.all_to_all(value_states, "head", split_axis=1, concat_axis=0, tiled=True),
    )
    q_heads = lax.all_to_all(queries, "head", split_axis=1, concat_axis=0, tiled=True)
    shard_tok = q_heads.shape[0]
    tile_count = shard_tok // TILE
    width = heads_local * DH
    local_pair = jnp.stack((k_heads, v_heads))

    n = cycle_size
    from_left2 = permute(local_pair, "blk", shift_pairs(n, 2))
    from_right2 = permute(local_pair, "blk", shift_pairs(n, -2))
    other_core = permute(local_pair, "blk", [(i, i ^ 1) for i in range(n)])
    blk_index = lax.axis_index("blk")
    core = blk_index % 2
    forward = jnp.where(core == 1, from_left2, from_right2)
    cross_route = [(i, i + 1) if i % 2 == 1 else (i, i - 1) for i in range(n)]
    cross_route = [(s, d % n) for s, d in cross_route]
    across = permute(forward, "blk", cross_route)
    other_left2 = permute(from_left2, "blk", [(i, i ^ 1) for i in range(n)])
    other_right2 = permute(from_right2, "blk", [(i, i ^ 1) for i in range(n)])
    window = jnp.concatenate(
        [local_pair, from_left2, from_right2, other_core, across, other_left2, other_right2], axis=1
    )

    shard_of = block_lists // tile_count
    offset = (shard_of - blk_index + REACH) % cycle_size
    table = jnp.array(PIECE_OF_OFFSET, dtype=jnp.int32)[core]
    slot_window = (table[offset] * tile_count + block_lists % tile_count).astype(jnp.int32)
    query_tile = blk_index * tile_count + jnp.arange(tile_count, dtype=jnp.int32)
    distance = (
        jnp.abs(tile_order[query_tile][:, None] - tile_order[block_lists]).astype(jnp.float32)
        / tile_order.shape[0]
    )
    head_index = lax.axis_index("head") * heads_local + jnp.arange(heads_local, dtype=jnp.int32)
    slopes = 8.0 * jnp.power(2.0, -8.0 * head_index.astype(jnp.float32) / H)
    bias = (slopes[None, None, :] * distance[:, :, None]).reshape(-1)
    scale = DH ** (-0.5)

    def kv_spec(which, c):
        return pl.BlockSpec((None, TILE, width), lambda i, sw, cnt, which=which, c=c: (which, sw[i * SLOTS + c], 0))

    in_specs = (
        [pl.BlockSpec(memory_space=pltpu.SMEM), pl.BlockSpec((TILE, width), lambda i, sw, cnt: (i, 0))]
        + [kv_spec(0, c) for c in range(SLOTS)]
        + [kv_spec(1, c) for c in range(SLOTS)]
    )
    grid_spec = pltpu.PrefetchScalarGridSpec(
        num_scalar_prefetch=2,
        grid=(tile_count,),
        in_specs=in_specs,
        out_specs=pl.BlockSpec((TILE, width), lambda i, sw, cnt: (i, 0)),
    )
    kernel = lambda *args: attention_kernel(*args, heads_local=heads_local, scale=scale)
    out = pl.pallas_call(
        kernel,
        grid_spec=grid_spec,
        out_shape=jax.ShapeDtypeStruct((shard_tok, width), jnp.bfloat16),
    )(slot_window.reshape(-1), block_counts.astype(jnp.int32), bias, q_heads, *([window] * (2 * SLOTS)))
    return lax.all_to_all(out, "head", split_axis=0, concat_axis=1, tiled=True)


def solution(mesh):
    in_specs = (
        P(("blk", "head"), None),
        P(("blk", "head"), None),
        P(("blk", "head"), None),
        P("blk", None),
        P("blk"),
        P(),
    )
    out_specs = P(("blk", "head"), None)
    return jax.shard_map(body, mesh=mesh, in_specs=in_specs, out_specs=out_specs, check_vma=False)
```

```python
import jax
import jax.numpy as jnp
from jax import lax
from jax.experimental import pallas as pl
from jax.experimental.pallas import tpu as pltpu
from jax.sharding import PartitionSpec as P

H = 48
DH = 128
TILE = 128
REACH = 3
SLOTS = 8

PIECE_OF_OFFSET = ((4, 1, 5, 0, 3, 2, 6), (5, 1, 3, 0, 6, 2, 4))


def permute(block, axis, route):
    return lax.ppermute(block, axis, route)


def shift_pairs(n, distance):
    return [(i, (i + distance) % n) for i in range(n)]


def attention_kernel(sw_ref, cnt_ref, bias_ref, q_ref, *refs, heads_local, scale):
    k_refs = refs[:SLOTS]
    v_refs = refs[SLOTS:2 * SLOTS]
    o_ref = refs[2 * SLOTS]
    i = pl.program_id(0)
    count = cnt_ref[i]
    for h in range(heads_local):
        cols = slice(h * DH, (h + 1) * DH)
        q = q_ref[:, cols]
        scores = []
        for c in range(SLOTS):
            s = jnp.dot(q, k_refs[c][cols, :], preferred_element_type=jnp.float32)
            s = s * scale
            s = s - bias_ref[(i * SLOTS + c) * heads_local + h]
            s = jnp.where(c < count, s, -1e30)
            scores.append(s)
        top = scores[0].max(axis=1, keepdims=True)
        for c in range(1, SLOTS):
            top = jnp.maximum(top, scores[c].max(axis=1, keepdims=True))
        total = jnp.zeros((TILE, 1), jnp.float32)
        acc = jnp.zeros((TILE, DH), jnp.float32)
        for c in range(SLOTS):
            w = jnp.exp(scores[c] - top).astype(jnp.bfloat16)
            total = total + w.astype(jnp.float32).sum(axis=1, keepdims=True)
            acc = acc + jnp.dot(w, v_refs[c][:, cols], preferred_element_type=jnp.float32)
        o_ref[:, cols] = (acc / total).astype(o_ref.dtype)


def exchange(local, axis, n):
    swap = [(i, i ^ 1) for i in range(n)]
    from_left2 = permute(local, "blk", shift_pairs(n, 2))
    from_right2 = permute(local, "blk", shift_pairs(n, -2))
    other_core = permute(local, "blk", swap)
    core = lax.axis_index("blk") % 2
    forward = jnp.where(core == 1, from_left2, from_right2)
    cross_route = [((i, (i + 1) % n) if i % 2 == 1 else (i, (i - 1) % n)) for i in range(n)]
    across = permute(forward, "blk", cross_route)
    other_left2 = permute(from_left2, "blk", swap)
    other_right2 = permute(from_right2, "blk", swap)
    pieces = [local, from_left2, from_right2, other_core, across, other_left2, other_right2]
    return jnp.concatenate(pieces, axis=axis)


def body(queries, key_states, value_states, block_lists, block_counts, tile_order):
    cycle_size = lax.axis_size("blk")
    group_size = lax.axis_size("head")
    heads_local = H // group_size
    k_heads = lax.all_to_all(key_states, "head", split_axis=1, concat_axis=0, tiled=True)
    k_window = exchange(k_heads.T, 1, cycle_size)
    v_heads = lax.all_to_all(value_states, "head", split_axis=1, concat_axis=0, tiled=True)
    v_window = exchange(v_heads, 0, cycle_size)
    q_heads = lax.all_to_all(queries, "head", split_axis=1, concat_axis=0, tiled=True)
    shard_tok = q_heads.shape[0]
    tile_count = shard_tok // TILE
    width = heads_local * DH

    blk_index = lax.axis_index("blk")
    core = blk_index % 2
    shard_of = block_lists // tile_count
    offset = (shard_of - blk_index + REACH) % cycle_size
    table = jnp.array(PIECE_OF_OFFSET, dtype=jnp.int32)[core]
    slot_window = (table[offset] * tile_count + block_lists % tile_count).astype(jnp.int32)
    query_tile = blk_index * tile_count + jnp.arange(tile_count, dtype=jnp.int32)
    distance = (
        jnp.abs(tile_order[query_tile][:, None] - tile_order[block_lists]).astype(jnp.float32)
        / tile_order.shape[0]
    )
    head_index = lax.axis_index("head") * heads_local + jnp.arange(heads_local, dtype=jnp.int32)
    slopes = 8.0 * jnp.power(2.0, -8.0 * head_index.astype(jnp.float32) / H)
    bias = (slopes[None, None, :] * distance[:, :, None]).reshape(-1)
    scale = DH ** (-0.5)

    k_specs = [
        pl.BlockSpec((width, TILE), lambda i, sw, cnt, c=c: (0, sw[i * SLOTS + c])) for c in range(SLOTS)
    ]
    v_specs = [
        pl.BlockSpec((TILE, width), lambda i, sw, cnt, c=c: (sw[i * SLOTS + c], 0)) for c in range(SLOTS)
    ]
    in_specs = (
        [pl.BlockSpec(memory_space=pltpu.SMEM), pl.BlockSpec((TILE, width), lambda i, sw, cnt: (i, 0))]
        + k_specs
        + v_specs
    )
    grid_spec = pltpu.PrefetchScalarGridSpec(
        num_scalar_prefetch=2,
        grid=(tile_count,),
        in_specs=in_specs,
        out_specs=pl.BlockSpec((TILE, width), lambda i, sw, cnt: (i, 0)),
    )
    kernel = lambda *args: attention_kernel(*args, heads_local=heads_local, scale=scale)
    out = pl.pallas_call(
        kernel,
        grid_spec=grid_spec,
        out_shape=jax.ShapeDtypeStruct((shard_tok, width), jnp.bfloat16),
    )(
        slot_window.reshape(-1),
        block_counts.astype(jnp.int32),
        bias,
        q_heads,
        *([k_window] * SLOTS),
        *([v_window] * SLOTS),
    )
    return lax.all_to_all(out, "head", split_axis=0, concat_axis=1, tiled=True)


def solution(mesh):
    in_specs = (
        P(("blk", "head"), None),
        P(("blk", "head"), None),
        P(("blk", "head"), None),
        P("blk", None),
        P("blk"),
        P(),
    )
    out_specs = P(("blk", "head"), None)
    return jax.shard_map(body, mesh=mesh, in_specs=in_specs, out_specs=out_specs, check_vma=False)
```

```python
import jax
import jax.numpy as jnp
from jax import lax
from jax.experimental import pallas as pl
from jax.experimental.pallas import tpu as pltpu
from jax.sharding import PartitionSpec as P

H = 48
DH = 128
TILE = 128
REACH = 3
SLOTS = 8

PIECE_OF_OFFSET = ((4, 1, 5, 0, 3, 2, 6), (5, 1, 3, 0, 6, 2, 4))


def permute(block, axis, route):
    return lax.ppermute(block, axis, route)


def shift_pairs(n, distance):
    return [(i, (i + distance) % n) for i in range(n)]


def attention_kernel(sw_ref, cnt_ref, bias_ref, q_ref, *refs, heads_local, scale):
    k_refs = refs[:SLOTS]
    v_refs = refs[SLOTS:2 * SLOTS]
    o_ref = refs[2 * SLOTS]
    i = pl.program_id(0)
    count = cnt_ref[i]
    for h in range(heads_local):
        cols = slice(h * DH, (h + 1) * DH)
        q = q_ref[:, cols]
        scores = []
        for c in range(SLOTS):
            s = jnp.dot(q, k_refs[c][cols, :], preferred_element_type=jnp.float32)
            s = s * scale
            s = s - bias_ref[(i * SLOTS + c) * heads_local + h]
            s = jnp.where(c < count, s, -1e30)
            scores.append(s)
        top = scores[0].max(axis=1, keepdims=True)
        for c in range(1, SLOTS):
            top = jnp.maximum(top, scores[c].max(axis=1, keepdims=True))
        total = jnp.zeros((TILE, 1), jnp.float32)
        acc = jnp.zeros((TILE, DH), jnp.float32)
        for c in range(SLOTS):
            w = jnp.exp(scores[c] - top).astype(jnp.bfloat16)
            total = total + w.astype(jnp.float32).sum(axis=1, keepdims=True)
            acc = acc + jnp.dot(w, v_refs[c][:, cols], preferred_element_type=jnp.float32)
        o_ref[:, cols] = (acc / total).astype(o_ref.dtype)


def detour(local, n, distance):
    group = 8
    crossing = group - 1 if distance > 0 else 1
    direct = [(i, (i + distance) % n) for i in range(n) if i % group != crossing]
    moved = permute(local, "blk", direct)
    step = group if distance > 0 else -group
    hop1 = permute(local, "blk", [(i, (i + step) % n) for i in range(n) if i % group == crossing])
    hop2 = permute(hop1, "blk", [(i, (i + distance - step) % n) for i in range(n) if i % group == crossing])
    arrived = (lax.axis_index("blk") - distance) % group == crossing
    return jnp.where(arrived, hop2, moved)


def exchange(local, axis, n):
    swap = [(i, i ^ 1) for i in range(n)]
    from_left2 = detour(local, n, 2)
    from_right2 = detour(local, n, -2)
    other_core = permute(local, "blk", swap)
    core = lax.axis_index("blk") % 2
    forward = jnp.where(core == 1, from_left2, from_right2)
    cross_route = [((i, (i + 1) % n) if i % 2 == 1 else (i, (i - 1) % n)) for i in range(n)]
    across = permute(forward, "blk", cross_route)
    other_left2 = permute(from_left2, "blk", swap)
    other_right2 = permute(from_right2, "blk", swap)
    pieces = [local, from_left2, from_right2, other_core, across, other_left2, other_right2]
    return jnp.concatenate(pieces, axis=axis)


def body(queries, key_states, value_states, block_lists, block_counts, tile_order):
    cycle_size = lax.axis_size("blk")
    group_size = lax.axis_size("head")
    heads_local = H // group_size
    k_heads = lax.all_to_all(key_states, "head", split_axis=1, concat_axis=0, tiled=True)
    k_window = exchange(k_heads.T, 1, cycle_size)
    v_heads = lax.all_to_all(value_states, "head", split_axis=1, concat_axis=0, tiled=True)
    v_window = exchange(v_heads, 0, cycle_size)
    q_heads = lax.all_to_all(queries, "head", split_axis=1, concat_axis=0, tiled=True)
    shard_tok = q_heads.shape[0]
    tile_count = shard_tok // TILE
    width = heads_local * DH

    blk_index = lax.axis_index("blk")
    core = blk_index % 2
    shard_of = block_lists // tile_count
    offset = (shard_of - blk_index + REACH) % cycle_size
    table = jnp.array(PIECE_OF_OFFSET, dtype=jnp.int32)[core]
    slot_window = (table[offset] * tile_count + block_lists % tile_count).astype(jnp.int32)
    query_tile = blk_index * tile_count + jnp.arange(tile_count, dtype=jnp.int32)
    distance = (
        jnp.abs(tile_order[query_tile][:, None] - tile_order[block_lists]).astype(jnp.float32)
        / tile_order.shape[0]
    )
    head_index = lax.axis_index("head") * heads_local + jnp.arange(heads_local, dtype=jnp.int32)
    slopes = 8.0 * jnp.power(2.0, -8.0 * head_index.astype(jnp.float32) / H)
    bias = (slopes[None, None, :] * distance[:, :, None]).reshape(-1)
    scale = DH ** (-0.5)

    k_specs = [
        pl.BlockSpec((width, TILE), lambda i, sw, cnt, c=c: (0, sw[i * SLOTS + c])) for c in range(SLOTS)
    ]
    v_specs = [
        pl.BlockSpec((TILE, width), lambda i, sw, cnt, c=c: (sw[i * SLOTS + c], 0)) for c in range(SLOTS)
    ]
    in_specs = (
        [pl.BlockSpec(memory_space=pltpu.SMEM), pl.BlockSpec((TILE, width), lambda i, sw, cnt: (i, 0))]
        + k_specs
        + v_specs
    )
    grid_spec = pltpu.PrefetchScalarGridSpec(
        num_scalar_prefetch=2,
        grid=(tile_count,),
        in_specs=in_specs,
        out_specs=pl.BlockSpec((TILE, width), lambda i, sw, cnt: (i, 0)),
    )
    kernel = lambda *args: attention_kernel(*args, heads_local=heads_local, scale=scale)
    out = pl.pallas_call(
        kernel,
        grid_spec=grid_spec,
        out_shape=jax.ShapeDtypeStruct((shard_tok, width), jnp.bfloat16),
    )(
        slot_window.reshape(-1),
        block_counts.astype(jnp.int32),
        bias,
        q_heads,
        *([k_window] * SLOTS),
        *([v_window] * SLOTS),
    )
    return lax.all_to_all(out, "head", split_axis=0, concat_axis=1, tiled=True)


def solution(mesh):
    in_specs = (
        P(("blk", "head"), None),
        P(("blk", "head"), None),
        P(("blk", "head"), None),
        P("blk", None),
        P("blk"),
        P(),
    )
    out_specs = P(("blk", "head"), None)
    return jax.shard_map(body, mesh=mesh, in_specs=in_specs, out_specs=out_specs, check_vma=False)
```

```python
import jax
import jax.numpy as jnp
from jax import lax
from jax.experimental import pallas as pl
from jax.experimental.pallas import tpu as pltpu
from jax.sharding import PartitionSpec as P

H = 48
DH = 128
TILE = 128
REACH = 3
SLOTS = 8
TILE_COUNT = 8

PIECE_OF_OFFSET = ((4, 1, 5, 0, 3, 2, 6), (5, 1, 3, 0, 6, 2, 4))


def permute(block, axis, route):
    return lax.ppermute(block, axis, route)


def shift_pairs(n, distance):
    return [(i, (i + distance) % n) for i in range(n)]


def attention_kernel(sw_ref, cnt_ref, bias_ref, q_ref, *refs, heads_local, scale, pieces):
    k_hbm = refs[:pieces]
    v_hbm = refs[pieces:2 * pieces]
    o_ref, k_buf, v_buf, sem = refs[2 * pieces:]
    i = pl.program_id(0)
    steps = pl.num_programs(0)
    parity = i % 2

    def copies(step, slot, c, p, j):
        k_copy = pltpu.make_async_copy(k_hbm[p].at[:, pl.ds(j * TILE, TILE)], k_buf.at[slot, c], sem.at[0, slot, c])
        v_copy = pltpu.make_async_copy(v_hbm[p].at[pl.ds(j * TILE, TILE), :], v_buf.at[slot, c], sem.at[1, slot, c])
        return k_copy, v_copy

    def start(step, slot):
        for c in range(SLOTS):
            code = sw_ref[step * SLOTS + c]
            p_code = code // TILE_COUNT
            j = code % TILE_COUNT
            for p in range(pieces):
                @pl.when(p_code == p)
                def _():
                    for copy in copies(step, slot, c, p, j):
                        copy.start()

    @pl.when(i == 0)
    def _():
        start(0, 0)

    @pl.when(i + 1 < steps)
    def _():
        start(i + 1, 1 - parity)

    for c in range(SLOTS):
        for copy in copies(i, parity, c, 0, 0):
            copy.wait()

    count = cnt_ref[i]
    for h in range(heads_local):
        cols = slice(h * DH, (h + 1) * DH)
        q = q_ref[:, cols]
        scores = []
        for c in range(SLOTS):
            s = jnp.dot(q, k_buf[parity, c, cols, :], preferred_element_type=jnp.float32)
            s = s * scale
            s = s - bias_ref[(i * SLOTS + c) * heads_local + h]
            s = jnp.where(c < count, s, -1e30)
            scores.append(s)
        top = scores[0].max(axis=1, keepdims=True)
        for c in range(1, SLOTS):
            top = jnp.maximum(top, scores[c].max(axis=1, keepdims=True))
        total = jnp.zeros((TILE, 1), jnp.float32)
        acc = jnp.zeros((TILE, DH), jnp.float32)
        for c in range(SLOTS):
            w = jnp.exp(scores[c] - top).astype(jnp.bfloat16)
            total = total + w.astype(jnp.float32).sum(axis=1, keepdims=True)
            acc = acc + jnp.dot(w, v_buf[parity, c, :, cols], preferred_element_type=jnp.float32)
        o_ref[:, cols] = (acc / total).astype(o_ref.dtype)


def exchange(local, axis, n):
    swap = [(i, i ^ 1) for i in range(n)]
    from_left2 = permute(local, "blk", shift_pairs(n, 2))
    from_right2 = permute(local, "blk", shift_pairs(n, -2))
    other_core = permute(local, "blk", swap)
    core = lax.axis_index("blk") % 2
    forward = jnp.where(core == 1, from_left2, from_right2)
    cross_route = [((i, (i + 1) % n) if i % 2 == 1 else (i, (i - 1) % n)) for i in range(n)]
    across = permute(forward, "blk", cross_route)
    other_left2 = permute(from_left2, "blk", swap)
    other_right2 = permute(from_right2, "blk", swap)
    return [local, from_left2, from_right2, other_core, across, other_left2, other_right2]


def body(queries, key_states, value_states, block_lists, block_counts, tile_order):
    cycle_size = lax.axis_size("blk")
    group_size = lax.axis_size("head")
    heads_local = H // group_size
    k_heads = lax.all_to_all(key_states, "head", split_axis=1, concat_axis=0, tiled=True)
    k_window = exchange(k_heads.T, 1, cycle_size)
    v_heads = lax.all_to_all(value_states, "head", split_axis=1, concat_axis=0, tiled=True)
    v_window = exchange(v_heads, 0, cycle_size)
    q_heads = lax.all_to_all(queries, "head", split_axis=1, concat_axis=0, tiled=True)
    shard_tok = q_heads.shape[0]
    tile_count = shard_tok // TILE
    width = heads_local * DH

    blk_index = lax.axis_index("blk")
    core = blk_index % 2
    shard_of = block_lists // tile_count
    offset = (shard_of - blk_index + REACH) % cycle_size
    table = jnp.array(PIECE_OF_OFFSET, dtype=jnp.int32)[core]
    slot_window = (table[offset] * tile_count + block_lists % tile_count).astype(jnp.int32)
    query_tile = blk_index * tile_count + jnp.arange(tile_count, dtype=jnp.int32)
    distance = (
        jnp.abs(tile_order[query_tile][:, None] - tile_order[block_lists]).astype(jnp.float32)
        / tile_order.shape[0]
    )
    head_index = lax.axis_index("head") * heads_local + jnp.arange(heads_local, dtype=jnp.int32)
    slopes = 8.0 * jnp.power(2.0, -8.0 * head_index.astype(jnp.float32) / H)
    bias = (slopes[None, None, :] * distance[:, :, None]).reshape(-1)
    scale = DH ** (-0.5)

    assert tile_count == TILE_COUNT
    pieces = len(k_window)
    any_spec = pl.BlockSpec(memory_space=pl.ANY)
    in_specs = (
        [pl.BlockSpec(memory_space=pltpu.SMEM), pl.BlockSpec((TILE, width), lambda i, sw, cnt: (i, 0))]
        + [any_spec] * (2 * pieces)
    )
    grid_spec = pltpu.PrefetchScalarGridSpec(
        num_scalar_prefetch=2,
        grid=(tile_count,),
        in_specs=in_specs,
        out_specs=pl.BlockSpec((TILE, width), lambda i, sw, cnt: (i, 0)),
        scratch_shapes=[
            pltpu.VMEM((2, SLOTS, width, TILE), jnp.bfloat16),
            pltpu.VMEM((2, SLOTS, TILE, width), jnp.bfloat16),
            pltpu.SemaphoreType.DMA((2, 2, SLOTS)),
        ],
    )
    kernel = lambda *args: attention_kernel(*args, heads_local=heads_local, scale=scale, pieces=pieces)
    out = pl.pallas_call(
        kernel,
        grid_spec=grid_spec,
        out_shape=jax.ShapeDtypeStruct((shard_tok, width), jnp.bfloat16),
        compiler_params=pltpu.CompilerParams(dimension_semantics=("arbitrary",)),
    )(
        slot_window.reshape(-1),
        block_counts.astype(jnp.int32),
        bias,
        q_heads,
        *k_window,
        *v_window,
    )
    return lax.all_to_all(out, "head", split_axis=0, concat_axis=1, tiled=True)


def solution(mesh):
    in_specs = (
        P(("blk", "head"), None),
        P(("blk", "head"), None),
        P(("blk", "head"), None),
        P("blk", None),
        P("blk"),
        P(),
    )
    out_specs = P(("blk", "head"), None)
    return jax.shard_map(body, mesh=mesh, in_specs=in_specs, out_specs=out_specs, check_vma=False)
```

```python
import jax
import jax.numpy as jnp
from jax import lax
from jax.experimental import pallas as pl
from jax.experimental.pallas import tpu as pltpu
from jax.sharding import PartitionSpec as P

H = 48
DH = 128
TILE = 128
REACH = 3
SLOTS = 8
TILE_COUNT = 8

PIECE_OF_OFFSET = ((4, 1, 5, 0, 3, 2, 6), (5, 1, 3, 0, 6, 2, 4))


def permute(block, axis, route):
    return lax.ppermute(block, axis, route)


def shift_pairs(n, distance):
    return [(i, (i + distance) % n) for i in range(n)]


def attention_kernel(sw_ref, cnt_ref, bias_ref, q_ref, *refs, heads_local, scale, pieces):
    k_hbm = refs[:pieces]
    v_hbm = refs[pieces:2 * pieces]
    o_ref, k_buf, v_buf, sem = refs[2 * pieces:]
    i = pl.program_id(0)
    steps = pl.num_programs(0)
    parity = i % 2

    def copies(step, slot, c, p, j):
        k_copy = pltpu.make_async_copy(
            k_hbm[p].at[:, pl.ds(j * TILE, TILE)], k_buf.at[slot, :, pl.ds(c * TILE, TILE)], sem.at[0, slot, c]
        )
        v_copy = pltpu.make_async_copy(
            v_hbm[p].at[pl.ds(j * TILE, TILE), :], v_buf.at[slot, pl.ds(c * TILE, TILE), :], sem.at[1, slot, c]
        )
        return k_copy, v_copy

    def start(step, slot):
        for c in range(SLOTS):
            code = sw_ref[step * SLOTS + c]
            p_code = code // TILE_COUNT
            j = code % TILE_COUNT
            for p in range(pieces):
                @pl.when(p_code == p)
                def _():
                    for copy in copies(step, slot, c, p, j):
                        copy.start()

    @pl.when(i == 0)
    def _():
        start(0, 0)

    @pl.when(i + 1 < steps)
    def _():
        start(i + 1, 1 - parity)

    for c in range(SLOTS):
        for copy in copies(i, parity, c, 0, 0):
            copy.wait()

    count = cnt_ref[i]
    keys = SLOTS * TILE
    valid = lax.broadcasted_iota(jnp.int32, (TILE, keys), 1) < count * TILE
    k_all = k_buf.at[parity]
    v_all = v_buf.at[parity]
    for h in range(heads_local):
        cols = slice(h * DH, (h + 1) * DH)
        s = jnp.dot(q_ref[:, cols], k_all[cols, :], preferred_element_type=jnp.float32)
        s = s * scale
        s = s - bias_ref[h : h + 1, :]
        s = jnp.where(valid, s, -1e30)
        top = s.max(axis=1, keepdims=True)
        w = jnp.exp(s - top).astype(jnp.bfloat16)
        total = w.astype(jnp.float32).sum(axis=1, keepdims=True)
        acc = jnp.dot(w, v_all[:, cols], preferred_element_type=jnp.float32)
        o_ref[:, cols] = (acc / total).astype(o_ref.dtype)


def exchange(local, axis, n):
    swap = [(i, i ^ 1) for i in range(n)]
    from_left2 = permute(local, "blk", shift_pairs(n, 2))
    from_right2 = permute(local, "blk", shift_pairs(n, -2))
    other_core = permute(local, "blk", swap)
    core = lax.axis_index("blk") % 2
    forward = jnp.where(core == 1, from_left2, from_right2)
    cross_route = [((i, (i + 1) % n) if i % 2 == 1 else (i, (i - 1) % n)) for i in range(n)]
    across = permute(forward, "blk", cross_route)
    other_left2 = permute(from_left2, "blk", swap)
    other_right2 = permute(from_right2, "blk", swap)
    return [local, from_left2, from_right2, other_core, across, other_left2, other_right2]


def body(queries, key_states, value_states, block_lists, block_counts, tile_order):
    cycle_size = lax.axis_size("blk")
    group_size = lax.axis_size("head")
    heads_local = H // group_size
    k_heads = lax.all_to_all(key_states, "head", split_axis=1, concat_axis=0, tiled=True)
    k_window = exchange(k_heads.T, 1, cycle_size)
    v_heads = lax.all_to_all(value_states, "head", split_axis=1, concat_axis=0, tiled=True)
    v_window = exchange(v_heads, 0, cycle_size)
    q_heads = lax.all_to_all(queries, "head", split_axis=1, concat_axis=0, tiled=True)
    shard_tok = q_heads.shape[0]
    tile_count = shard_tok // TILE
    width = heads_local * DH

    blk_index = lax.axis_index("blk")
    core = blk_index % 2
    shard_of = block_lists // tile_count
    offset = (shard_of - blk_index + REACH) % cycle_size
    table = jnp.array(PIECE_OF_OFFSET, dtype=jnp.int32)[core]
    slot_window = (table[offset] * tile_count + block_lists % tile_count).astype(jnp.int32)
    query_tile = blk_index * tile_count + jnp.arange(tile_count, dtype=jnp.int32)
    distance = (
        jnp.abs(tile_order[query_tile][:, None] - tile_order[block_lists]).astype(jnp.float32)
        / tile_order.shape[0]
    )
    head_index = lax.axis_index("head") * heads_local + jnp.arange(heads_local, dtype=jnp.int32)
    slopes = 8.0 * jnp.power(2.0, -8.0 * head_index.astype(jnp.float32) / H)
    bias = slopes[None, :, None, None] * distance[:, None, :, None]
    bias = jnp.broadcast_to(bias, (tile_count, heads_local, SLOTS, TILE)).reshape(tile_count, heads_local, SLOTS * TILE)
    scale = DH ** (-0.5)

    assert tile_count == TILE_COUNT
    pieces = len(k_window)
    any_spec = pl.BlockSpec(memory_space=pl.ANY)
    in_specs = (
        [
            pl.BlockSpec((None, heads_local, SLOTS * TILE), lambda i, sw, cnt: (i, 0, 0)),
            pl.BlockSpec((TILE, width), lambda i, sw, cnt: (i, 0)),
        ]
        + [any_spec] * (2 * pieces)
    )
    grid_spec = pltpu.PrefetchScalarGridSpec(
        num_scalar_prefetch=2,
        grid=(tile_count,),
        in_specs=in_specs,
        out_specs=pl.BlockSpec((TILE, width), lambda i, sw, cnt: (i, 0)),
        scratch_shapes=[
            pltpu.VMEM((2, width, SLOTS * TILE), jnp.bfloat16),
            pltpu.VMEM((2, SLOTS * TILE, width), jnp.bfloat16),
            pltpu.SemaphoreType.DMA((2, 2, SLOTS)),
        ],
    )
    kernel = lambda *args: attention_kernel(*args, heads_local=heads_local, scale=scale, pieces=pieces)
    out = pl.pallas_call(
        kernel,
        grid_spec=grid_spec,
        out_shape=jax.ShapeDtypeStruct((shard_tok, width), jnp.bfloat16),
        compiler_params=pltpu.CompilerParams(dimension_semantics=("arbitrary",)),
    )(
        slot_window.reshape(-1),
        block_counts.astype(jnp.int32),
        bias,
        q_heads,
        *k_window,
        *v_window,
    )
    return lax.all_to_all(out, "head", split_axis=0, concat_axis=1, tiled=True)


def solution(mesh):
    in_specs = (
        P(("blk", "head"), None),
        P(("blk", "head"), None),
        P(("blk", "head"), None),
        P("blk", None),
        P("blk"),
        P(),
    )
    out_specs = P(("blk", "head"), None)
    return jax.shard_map(body, mesh=mesh, in_specs=in_specs, out_specs=out_specs, check_vma=False)
```

```python
import jax
import jax.numpy as jnp
from jax import lax
from jax.experimental import pallas as pl
from jax.experimental.pallas import tpu as pltpu
from jax.sharding import PartitionSpec as P

H = 48
DH = 128
TILE = 128
REACH = 3
SLOTS = 8
TILE_COUNT = 8

PIECE_OF_OFFSET = ((4, 1, 6, 0, 3, 2, 7), (6, 1, 3, 0, 7, 2, 5))


def permute(block, axis, route):
    return lax.ppermute(block, axis, route)


def shift_pairs(n, distance):
    return [(i, (i + distance) % n) for i in range(n)]


def attention_kernel(sw_ref, cnt_ref, bias_ref, q_ref, *refs, heads_local, scale, pieces):
    k_hbm = refs[:pieces]
    v_hbm = refs[pieces:2 * pieces]
    o_ref, k_buf, v_buf, sem = refs[2 * pieces:]
    i = pl.program_id(0)
    steps = pl.num_programs(0)
    parity = i % 2

    def copies(step, slot, c, p, j):
        k_copy = pltpu.make_async_copy(
            k_hbm[p].at[:, pl.ds(j * TILE, TILE)], k_buf.at[slot, :, pl.ds(c * TILE, TILE)], sem.at[0, slot, c]
        )
        v_copy = pltpu.make_async_copy(
            v_hbm[p].at[pl.ds(j * TILE, TILE), :], v_buf.at[slot, pl.ds(c * TILE, TILE), :], sem.at[1, slot, c]
        )
        return k_copy, v_copy

    def start(step, slot):
        for c in range(SLOTS):
            code = sw_ref[step * SLOTS + c]
            p_code = code // TILE_COUNT
            j = code % TILE_COUNT
            for p in range(pieces):
                @pl.when(p_code == p)
                def _():
                    for copy in copies(step, slot, c, p, j):
                        copy.start()

    @pl.when(i == 0)
    def _():
        start(0, 0)

    @pl.when(i + 1 < steps)
    def _():
        start(i + 1, 1 - parity)

    for c in range(SLOTS):
        for copy in copies(i, parity, c, 0, 0):
            copy.wait()

    count = cnt_ref[i]
    keys = SLOTS * TILE
    valid = lax.broadcasted_iota(jnp.int32, (TILE, keys), 1) < count * TILE
    k_all = k_buf.at[parity]
    v_all = v_buf.at[parity]
    for h in range(heads_local):
        cols = slice(h * DH, (h + 1) * DH)
        s = jnp.dot(q_ref[:, cols], k_all[cols, :], preferred_element_type=jnp.float32)
        s = s * scale
        s = s - bias_ref[h : h + 1, :]
        s = jnp.where(valid, s, -1e30)
        top = s.max(axis=1, keepdims=True)
        w = jnp.exp(s - top).astype(jnp.bfloat16)
        total = w.astype(jnp.float32).sum(axis=1, keepdims=True)
        acc = jnp.dot(w, v_all[:, cols], preferred_element_type=jnp.float32)
        o_ref[:, cols] = (acc / total).astype(o_ref.dtype)


def exchange(local, axis, n):
    swap = [(i, i ^ 1) for i in range(n)]
    from_left2 = permute(local, "blk", shift_pairs(n, 2))
    from_right2 = permute(local, "blk", shift_pairs(n, -2))
    other_core = permute(local, "blk", swap)
    odd_ahead = permute(from_left2, "blk", [(i, (i + 1) % n) for i in range(1, n, 2)])
    even_back = permute(from_right2, "blk", [(i, (i - 1) % n) for i in range(0, n, 2)])
    other_left2 = permute(from_left2, "blk", swap)
    other_right2 = permute(from_right2, "blk", swap)
    return [local, from_left2, from_right2, other_core, odd_ahead, even_back, other_left2, other_right2]


def body(queries, key_states, value_states, block_lists, block_counts, tile_order):
    cycle_size = lax.axis_size("blk")
    group_size = lax.axis_size("head")
    heads_local = H // group_size
    k_heads = lax.all_to_all(key_states, "head", split_axis=1, concat_axis=0, tiled=True)
    k_window = exchange(k_heads.T, 1, cycle_size)
    v_heads = lax.all_to_all(value_states, "head", split_axis=1, concat_axis=0, tiled=True)
    v_window = exchange(v_heads, 0, cycle_size)
    q_heads = lax.all_to_all(queries, "head", split_axis=1, concat_axis=0, tiled=True)
    shard_tok = q_heads.shape[0]
    tile_count = shard_tok // TILE
    width = heads_local * DH

    blk_index = lax.axis_index("blk")
    core = blk_index % 2
    shard_of = block_lists // tile_count
    offset = (shard_of - blk_index + REACH) % cycle_size
    table = jnp.array(PIECE_OF_OFFSET, dtype=jnp.int32)[core]
    slot_window = (table[offset] * tile_count + block_lists % tile_count).astype(jnp.int32)
    query_tile = blk_index * tile_count + jnp.arange(tile_count, dtype=jnp.int32)
    distance = (
        jnp.abs(tile_order[query_tile][:, None] - tile_order[block_lists]).astype(jnp.float32)
        / tile_order.shape[0]
    )
    head_index = lax.axis_index("head") * heads_local + jnp.arange(heads_local, dtype=jnp.int32)
    slopes = 8.0 * jnp.power(2.0, -8.0 * head_index.astype(jnp.float32) / H)
    bias = slopes[None, :, None, None] * distance[:, None, :, None]
    bias = jnp.broadcast_to(bias, (tile_count, heads_local, SLOTS, TILE)).reshape(tile_count, heads_local, SLOTS * TILE)
    scale = DH ** (-0.5)

    assert tile_count == TILE_COUNT
    pieces = len(k_window)
    any_spec = pl.BlockSpec(memory_space=pl.ANY)
    in_specs = (
        [
            pl.BlockSpec((None, heads_local, SLOTS * TILE), lambda i, sw, cnt: (i, 0, 0)),
            pl.BlockSpec((TILE, width), lambda i, sw, cnt: (i, 0)),
        ]
        + [any_spec] * (2 * pieces)
    )
    grid_spec = pltpu.PrefetchScalarGridSpec(
        num_scalar_prefetch=2,
        grid=(tile_count,),
        in_specs=in_specs,
        out_specs=pl.BlockSpec((TILE, width), lambda i, sw, cnt: (i, 0)),
        scratch_shapes=[
            pltpu.VMEM((2, width, SLOTS * TILE), jnp.bfloat16),
            pltpu.VMEM((2, SLOTS * TILE, width), jnp.bfloat16),
            pltpu.SemaphoreType.DMA((2, 2, SLOTS)),
        ],
    )
    kernel = lambda *args: attention_kernel(*args, heads_local=heads_local, scale=scale, pieces=pieces)
    out = pl.pallas_call(
        kernel,
        grid_spec=grid_spec,
        out_shape=jax.ShapeDtypeStruct((shard_tok, width), jnp.bfloat16),
        compiler_params=pltpu.CompilerParams(dimension_semantics=("arbitrary",)),
    )(
        slot_window.reshape(-1),
        block_counts.astype(jnp.int32),
        bias,
        q_heads,
        *k_window,
        *v_window,
    )
    return lax.all_to_all(out, "head", split_axis=0, concat_axis=1, tiled=True)


def solution(mesh):
    in_specs = (
        P(("blk", "head"), None),
        P(("blk", "head"), None),
        P(("blk", "head"), None),
        P("blk", None),
        P("blk"),
        P(),
    )
    out_specs = P(("blk", "head"), None)
    return jax.shard_map(body, mesh=mesh, in_specs=in_specs, out_specs=out_specs, check_vma=False)
```

```python
import jax
import jax.numpy as jnp
from jax import lax
from jax.experimental import pallas as pl
from jax.experimental.pallas import tpu as pltpu
from jax.sharding import PartitionSpec as P

H = 48
DH = 128
TILE = 128
REACH = 3
SLOTS = 8
TILE_COUNT = 8

PIECE_OF_OFFSET = ((4, 1, 6, 0, 3, 2, 7), (6, 1, 3, 0, 7, 2, 5))


def permute(block, axis, route):
    return lax.ppermute(block, axis, route)


def shift_pairs(n, distance):
    return [(i, (i + distance) % n) for i in range(n)]


def attention_kernel(sw_ref, cnt_ref, bias_ref, q_ref, *refs, heads_local, scale, pieces):
    k_hbm = refs[:pieces]
    v_hbm = refs[pieces:2 * pieces]
    o_ref, k_buf, v_buf, sem = refs[2 * pieces:]
    i = pl.program_id(0)
    steps = pl.num_programs(0)
    parity = i % 2

    def copies(step, slot, c, p, j):
        k_copy = pltpu.make_async_copy(
            k_hbm[p].at[:, pl.ds(j * TILE, TILE)], k_buf.at[slot, :, pl.ds(c * TILE, TILE)], sem.at[0, slot, c]
        )
        v_copy = pltpu.make_async_copy(
            v_hbm[p].at[pl.ds(j * TILE, TILE), :], v_buf.at[slot, pl.ds(c * TILE, TILE), :], sem.at[1, slot, c]
        )
        return k_copy, v_copy

    def start(step, slot):
        for c in range(SLOTS):
            code = sw_ref[step * SLOTS + c]
            p_code = code // TILE_COUNT
            j = code % TILE_COUNT
            for p in range(pieces):
                @pl.when(p_code == p)
                def _():
                    for copy in copies(step, slot, c, p, j):
                        copy.start()

    @pl.when(i == 0)
    def _():
        start(0, 0)

    @pl.when(i + 1 < steps)
    def _():
        start(i + 1, 1 - parity)

    for c in range(SLOTS):
        for copy in copies(i, parity, c, 0, 0):
            copy.wait()

    count = cnt_ref[i]
    keys = SLOTS * TILE
    valid = lax.broadcasted_iota(jnp.int32, (TILE, keys), 1) < count * TILE
    k_all = k_buf.at[parity]
    v_all = v_buf.at[parity]
    for h in range(heads_local):
        cols = slice(h * DH, (h + 1) * DH)
        s = jnp.dot(q_ref[:, cols], k_all[cols, :], preferred_element_type=jnp.float32)
        s = s * scale
        s = s - bias_ref[h : h + 1, :]
        s = jnp.where(valid, s, -1e30)
        top = s.max(axis=1, keepdims=True)
        w = jnp.exp(s - top).astype(jnp.bfloat16)
        total = w.astype(jnp.float32).sum(axis=1, keepdims=True)
        acc = jnp.dot(w, v_all[:, cols], preferred_element_type=jnp.float32)
        o_ref[:, cols] = (acc / total).astype(o_ref.dtype)


def exchange(local, axis, n):
    swap = [(i, i ^ 1) for i in range(n)]
    from_left2 = permute(local, "blk", shift_pairs(n, 2))
    from_right2 = permute(local, "blk", shift_pairs(n, -2))
    other_core = permute(local, "blk", swap)
    odd_ahead = permute(from_left2, "blk", [(i, (i + 1) % n) for i in range(1, n, 2)])
    even_back = permute(from_right2, "blk", [(i, (i - 1) % n) for i in range(0, n, 2)])
    other_left2 = permute(from_left2, "blk", swap)
    other_right2 = permute(from_right2, "blk", swap)
    return [local, from_left2, from_right2, other_core, odd_ahead, even_back, other_left2, other_right2]


def body(queries, key_states, value_states, block_lists, block_counts, tile_order):
    cycle_size = lax.axis_size("blk")
    group_size = lax.axis_size("head")
    heads_local = H // group_size
    q_heads = lax.all_to_all(queries, "head", split_axis=1, concat_axis=0, tiled=True)
    q_heads, key_states = lax.optimization_barrier((q_heads, key_states))
    k_heads = lax.all_to_all(key_states, "head", split_axis=1, concat_axis=0, tiled=True)
    k_window = exchange(k_heads.T, 1, cycle_size)
    v_heads = lax.all_to_all(value_states, "head", split_axis=1, concat_axis=0, tiled=True)
    v_window = exchange(v_heads, 0, cycle_size)
    shard_tok = q_heads.shape[0]
    tile_count = shard_tok // TILE
    width = heads_local * DH

    blk_index = lax.axis_index("blk")
    core = blk_index % 2
    shard_of = block_lists // tile_count
    offset = (shard_of - blk_index + REACH) % cycle_size
    table = jnp.array(PIECE_OF_OFFSET, dtype=jnp.int32)[core]
    slot_window = (table[offset] * tile_count + block_lists % tile_count).astype(jnp.int32)
    query_tile = blk_index * tile_count + jnp.arange(tile_count, dtype=jnp.int32)
    distance = (
        jnp.abs(tile_order[query_tile][:, None] - tile_order[block_lists]).astype(jnp.float32)
        / tile_order.shape[0]
    )
    head_index = lax.axis_index("head") * heads_local + jnp.arange(heads_local, dtype=jnp.int32)
    slopes = 8.0 * jnp.power(2.0, -8.0 * head_index.astype(jnp.float32) / H)
    bias = slopes[None, :, None, None] * distance[:, None, :, None]
    bias = jnp.broadcast_to(bias, (tile_count, heads_local, SLOTS, TILE)).reshape(tile_count, heads_local, SLOTS * TILE)
    scale = DH ** (-0.5)

    assert tile_count == TILE_COUNT
    pieces = len(k_window)
    any_spec = pl.BlockSpec(memory_space=pl.ANY)
    in_specs = (
        [
            pl.BlockSpec((None, heads_local, SLOTS * TILE), lambda i, sw, cnt: (i, 0, 0)),
            pl.BlockSpec((TILE, width), lambda i, sw, cnt: (i, 0)),
        ]
        + [any_spec] * (2 * pieces)
    )
    grid_spec = pltpu.PrefetchScalarGridSpec(
        num_scalar_prefetch=2,
        grid=(tile_count,),
        in_specs=in_specs,
        out_specs=pl.BlockSpec((TILE, width), lambda i, sw, cnt: (i, 0)),
        scratch_shapes=[
            pltpu.VMEM((2, width, SLOTS * TILE), jnp.bfloat16),
            pltpu.VMEM((2, SLOTS * TILE, width), jnp.bfloat16),
            pltpu.SemaphoreType.DMA((2, 2, SLOTS)),
        ],
    )
    kernel = lambda *args: attention_kernel(*args, heads_local=heads_local, scale=scale, pieces=pieces)
    out = pl.pallas_call(
        kernel,
        grid_spec=grid_spec,
        out_shape=jax.ShapeDtypeStruct((shard_tok, width), jnp.bfloat16),
        compiler_params=pltpu.CompilerParams(dimension_semantics=("arbitrary",)),
    )(
        slot_window.reshape(-1),
        block_counts.astype(jnp.int32),
        bias,
        q_heads,
        *k_window,
        *v_window,
    )
    return lax.all_to_all(out, "head", split_axis=0, concat_axis=1, tiled=True)


def solution(mesh):
    in_specs = (
        P(("blk", "head"), None),
        P(("blk", "head"), None),
        P(("blk", "head"), None),
        P("blk", None),
        P("blk"),
        P(),
    )
    out_specs = P(("blk", "head"), None)
    return jax.shard_map(body, mesh=mesh, in_specs=in_specs, out_specs=out_specs, check_vma=False)
```

```python
import jax
import jax.numpy as jnp
from jax import lax
from jax.experimental import pallas as pl
from jax.experimental.pallas import tpu as pltpu
from jax.sharding import PartitionSpec as P

H = 48
DH = 128
TILE = 128
REACH = 3
SLOTS = 8
TILE_COUNT = 8

PIECE_OF_OFFSET = ((4, 1, 6, 0, 3, 2, 7), (6, 1, 3, 0, 7, 2, 5))


def permute(block, axis, route):
    return lax.ppermute(block, axis, route)


def shift_pairs(n, distance):
    return [(i, (i + distance) % n) for i in range(n)]


def attention_kernel(sw_ref, cnt_ref, bias_ref, q_ref, *refs, heads_local, scale, pieces):
    k_hbm = refs[:pieces]
    v_hbm = refs[pieces:2 * pieces]
    o_ref, k_buf, v_buf, sem = refs[2 * pieces:]
    i = pl.program_id(0)
    steps = pl.num_programs(0)
    parity = i % 2

    def copies(step, slot, c, p, j):
        k_copy = pltpu.make_async_copy(
            k_hbm[p].at[:, pl.ds(j * TILE, TILE)], k_buf.at[slot, :, pl.ds(c * TILE, TILE)], sem.at[0, slot, c]
        )
        v_copy = pltpu.make_async_copy(
            v_hbm[p].at[pl.ds(j * TILE, TILE), :], v_buf.at[slot, pl.ds(c * TILE, TILE), :], sem.at[1, slot, c]
        )
        return k_copy, v_copy

    def start(step, slot):
        for c in range(SLOTS):
            code = sw_ref[step * SLOTS + c]
            p_code = code // TILE_COUNT
            j = code % TILE_COUNT
            for p in range(pieces):
                @pl.when(p_code == p)
                def _():
                    for copy in copies(step, slot, c, p, j):
                        copy.start()

    @pl.when(i == 0)
    def _():
        start(0, 0)

    @pl.when(i + 1 < steps)
    def _():
        start(i + 1, 1 - parity)

    for c in range(SLOTS):
        for copy in copies(i, parity, c, 0, 0):
            copy.wait()

    count = cnt_ref[i]
    keys = SLOTS * TILE
    valid = lax.broadcasted_iota(jnp.int32, (TILE, keys), 1) < count * TILE
    k_all = k_buf.at[parity]
    v_all = v_buf.at[parity]
    for h in range(heads_local):
        cols = slice(h * DH, (h + 1) * DH)
        s = jnp.dot(q_ref[:, cols], k_all[cols, :], preferred_element_type=jnp.float32)
        s = s * scale
        s = s - bias_ref[h : h + 1, :]
        s = jnp.where(valid, s, -1e30)
        top = s.max(axis=1, keepdims=True)
        w = jnp.exp(s - top).astype(jnp.bfloat16)
        total = w.astype(jnp.float32).sum(axis=1, keepdims=True)
        acc = jnp.dot(w, v_all[:, cols], preferred_element_type=jnp.float32)
        o_ref[:, cols] = (acc / total).astype(o_ref.dtype)


def exchange(local, axis, n):
    swap = [(i, i ^ 1) for i in range(n)]
    from_left2 = permute(local, "blk", shift_pairs(n, 2))
    from_right2 = permute(local, "blk", shift_pairs(n, -2))
    other_core = permute(local, "blk", swap)
    odd_ahead = permute(from_left2, "blk", [(i, (i + 1) % n) for i in range(1, n, 2)])
    even_back = permute(from_right2, "blk", [(i, (i - 1) % n) for i in range(0, n, 2)])
    other_left2 = permute(from_left2, "blk", swap)
    other_right2 = permute(from_right2, "blk", swap)
    return [local, from_left2, from_right2, other_core, odd_ahead, even_back, other_left2, other_right2]


def body(queries, key_states, value_states, block_lists, block_counts, tile_order):
    cycle_size = lax.axis_size("blk")
    group_size = lax.axis_size("head")
    heads_local = H // group_size
    stacked = jnp.stack((queries, key_states, value_states))
    q_heads, k_heads, v_heads = lax.all_to_all(stacked, "head", split_axis=2, concat_axis=1, tiled=True)
    k_window = exchange(k_heads.T, 1, cycle_size)
    v_window = exchange(v_heads, 0, cycle_size)
    shard_tok = q_heads.shape[0]
    tile_count = shard_tok // TILE
    width = heads_local * DH

    blk_index = lax.axis_index("blk")
    core = blk_index % 2
    shard_of = block_lists // tile_count
    offset = (shard_of - blk_index + REACH) % cycle_size
    table = jnp.array(PIECE_OF_OFFSET, dtype=jnp.int32)[core]
    slot_window = (table[offset] * tile_count + block_lists % tile_count).astype(jnp.int32)
    query_tile = blk_index * tile_count + jnp.arange(tile_count, dtype=jnp.int32)
    distance = (
        jnp.abs(tile_order[query_tile][:, None] - tile_order[block_lists]).astype(jnp.float32)
        / tile_order.shape[0]
    )
    head_index = lax.axis_index("head") * heads_local + jnp.arange(heads_local, dtype=jnp.int32)
    slopes = 8.0 * jnp.power(2.0, -8.0 * head_index.astype(jnp.float32) / H)
    bias = slopes[None, :, None, None] * distance[:, None, :, None]
    bias = jnp.broadcast_to(bias, (tile_count, heads_local, SLOTS, TILE)).reshape(tile_count, heads_local, SLOTS * TILE)
    scale = DH ** (-0.5)

    assert tile_count == TILE_COUNT
    pieces = len(k_window)
    any_spec = pl.BlockSpec(memory_space=pl.ANY)
    in_specs = (
        [
            pl.BlockSpec((None, heads_local, SLOTS * TILE), lambda i, sw, cnt: (i, 0, 0)),
            pl.BlockSpec((TILE, width), lambda i, sw, cnt: (i, 0)),
        ]
        + [any_spec] * (2 * pieces)
    )
    grid_spec = pltpu.PrefetchScalarGridSpec(
        num_scalar_prefetch=2,
        grid=(tile_count,),
        in_specs=in_specs,
        out_specs=pl.BlockSpec((TILE, width), lambda i, sw, cnt: (i, 0)),
        scratch_shapes=[
            pltpu.VMEM((2, width, SLOTS * TILE), jnp.bfloat16),
            pltpu.VMEM((2, SLOTS * TILE, width), jnp.bfloat16),
            pltpu.SemaphoreType.DMA((2, 2, SLOTS)),
        ],
    )
    kernel = lambda *args: attention_kernel(*args, heads_local=heads_local, scale=scale, pieces=pieces)
    out = pl.pallas_call(
        kernel,
        grid_spec=grid_spec,
        out_shape=jax.ShapeDtypeStruct((shard_tok, width), jnp.bfloat16),
        compiler_params=pltpu.CompilerParams(dimension_semantics=("arbitrary",)),
    )(
        slot_window.reshape(-1),
        block_counts.astype(jnp.int32),
        bias,
        q_heads,
        *k_window,
        *v_window,
    )
    return lax.all_to_all(out, "head", split_axis=0, concat_axis=1, tiled=True)


def solution(mesh):
    in_specs = (
        P(("blk", "head"), None),
        P(("blk", "head"), None),
        P(("blk", "head"), None),
        P("blk", None),
        P("blk"),
        P(),
    )
    out_specs = P(("blk", "head"), None)
    return jax.shard_map(body, mesh=mesh, in_specs=in_specs, out_specs=out_specs, check_vma=False)
```

```python
import jax
import jax.numpy as jnp
from jax import lax
from jax.experimental import pallas as pl
from jax.experimental.pallas import tpu as pltpu
from jax.sharding import PartitionSpec as P

H = 48
DH = 128
TILE = 128
REACH = 3
SLOTS = 8
TILE_COUNT = 8

PIECE_OF_OFFSET = ((4, 1, 5, 0, 3, 2, 6), (5, 1, 3, 0, 6, 2, 4))


def permute(block, axis, route):
    return lax.ppermute(block, axis, route)


def shift_pairs(n, distance):
    return [(i, (i + distance) % n) for i in range(n)]


def attention_kernel(sw_ref, cnt_ref, bias_ref, q_ref, *refs, heads_local, scale, pieces):
    k_hbm = refs[:pieces]
    v_hbm = refs[pieces:2 * pieces]
    o_ref, k_buf, v_buf, sem = refs[2 * pieces:]
    i = pl.program_id(0)
    steps = pl.num_programs(0)
    parity = i % 2

    def copies(step, slot, c, p, j):
        k_copy = pltpu.make_async_copy(
            k_hbm[p].at[:, pl.ds(j * TILE, TILE)], k_buf.at[slot, :, pl.ds(c * TILE, TILE)], sem.at[0, slot, c]
        )
        v_copy = pltpu.make_async_copy(
            v_hbm[p].at[pl.ds(j * TILE, TILE), :], v_buf.at[slot, pl.ds(c * TILE, TILE), :], sem.at[1, slot, c]
        )
        return k_copy, v_copy

    def start(step, slot):
        for c in range(SLOTS):
            code = sw_ref[step * SLOTS + c]
            p_code = code // TILE_COUNT
            j = code % TILE_COUNT
            for p in range(pieces):
                @pl.when(jnp.logical_and(p_code == p, c < cnt_ref[step]))
                def _():
                    for copy in copies(step, slot, c, p, j):
                        copy.start()

    @pl.when(i == 0)
    def _():
        v_buf[...] = jnp.zeros(v_buf.shape, v_buf.dtype)
        start(0, 0)

    @pl.when(i + 1 < steps)
    def _():
        start(i + 1, 1 - parity)

    for c in range(SLOTS):
        @pl.when(c < cnt_ref[i])
        def _():
            for copy in copies(i, parity, c, 0, 0):
                copy.wait()

    count = cnt_ref[i]
    keys = SLOTS * TILE
    valid = lax.broadcasted_iota(jnp.int32, (TILE, keys), 1) < count * TILE
    k_all = k_buf.at[parity]
    v_all = v_buf.at[parity]
    for h in range(heads_local):
        cols = slice(h * DH, (h + 1) * DH)
        s = jnp.dot(q_ref[:, cols], k_all[cols, :], preferred_element_type=jnp.float32)
        s = s * scale
        s = s - bias_ref[h : h + 1, :]
        s = jnp.where(valid, s, -1e30)
        top = s.max(axis=1, keepdims=True)
        w = jnp.exp(s - top).astype(jnp.bfloat16)
        total = w.astype(jnp.float32).sum(axis=1, keepdims=True)
        acc = jnp.dot(w, v_all[:, cols], preferred_element_type=jnp.float32)
        o_ref[:, cols] = (acc / total).astype(o_ref.dtype)


def exchange(local, axis, n):
    swap = [(i, i ^ 1) for i in range(n)]
    from_left2 = permute(local, "blk", shift_pairs(n, 2))
    from_right2 = permute(local, "blk", shift_pairs(n, -2))
    other_core = permute(local, "blk", swap)
    core = lax.axis_index("blk") % 2
    forward = jnp.where(core == 1, from_left2, from_right2)
    cross_route = [((i, (i + 1) % n) if i % 2 == 1 else (i, (i - 1) % n)) for i in range(n)]
    across = permute(forward, "blk", cross_route)
    other_left2 = permute(from_left2, "blk", swap)
    other_right2 = permute(from_right2, "blk", swap)
    return [local, from_left2, from_right2, other_core, across, other_left2, other_right2]


def body(queries, key_states, value_states, block_lists, block_counts, tile_order):
    cycle_size = lax.axis_size("blk")
    group_size = lax.axis_size("head")
    heads_local = H // group_size
    k_heads = lax.all_to_all(key_states, "head", split_axis=1, concat_axis=0, tiled=True)
    k_window = exchange(k_heads.T, 1, cycle_size)
    v_heads = lax.all_to_all(value_states, "head", split_axis=1, concat_axis=0, tiled=True)
    v_window = exchange(v_heads, 0, cycle_size)
    q_heads = lax.all_to_all(queries, "head", split_axis=1, concat_axis=0, tiled=True)
    shard_tok = q_heads.shape[0]
    tile_count = shard_tok // TILE
    width = heads_local * DH

    blk_index = lax.axis_index("blk")
    core = blk_index % 2
    shard_of = block_lists // tile_count
    offset = (shard_of - blk_index + REACH) % cycle_size
    table = jnp.array(PIECE_OF_OFFSET, dtype=jnp.int32)[core]
    slot_window = (table[offset] * tile_count + block_lists % tile_count).astype(jnp.int32)
    query_tile = blk_index * tile_count + jnp.arange(tile_count, dtype=jnp.int32)
    distance = (
        jnp.abs(tile_order[query_tile][:, None] - tile_order[block_lists]).astype(jnp.float32)
        / tile_order.shape[0]
    )
    head_index = lax.axis_index("head") * heads_local + jnp.arange(heads_local, dtype=jnp.int32)
    slopes = 8.0 * jnp.power(2.0, -8.0 * head_index.astype(jnp.float32) / H)
    bias = slopes[None, :, None, None] * distance[:, None, :, None]
    bias = jnp.broadcast_to(bias, (tile_count, heads_local, SLOTS, TILE)).reshape(tile_count, heads_local, SLOTS * TILE)
    scale = DH ** (-0.5)

    assert tile_count == TILE_COUNT
    pieces = len(k_window)
    any_spec = pl.BlockSpec(memory_space=pl.ANY)
    in_specs = (
        [
            pl.BlockSpec((None, heads_local, SLOTS * TILE), lambda i, sw, cnt: (i, 0, 0)),
            pl.BlockSpec((TILE, width), lambda i, sw, cnt: (i, 0)),
        ]
        + [any_spec] * (2 * pieces)
    )
    grid_spec = pltpu.PrefetchScalarGridSpec(
        num_scalar_prefetch=2,
        grid=(tile_count,),
        in_specs=in_specs,
        out_specs=pl.BlockSpec((TILE, width), lambda i, sw, cnt: (i, 0)),
        scratch_shapes=[
            pltpu.VMEM((2, width, SLOTS * TILE), jnp.bfloat16),
            pltpu.VMEM((2, SLOTS * TILE, width), jnp.bfloat16),
            pltpu.SemaphoreType.DMA((2, 2, SLOTS)),
        ],
    )
    kernel = lambda *args: attention_kernel(*args, heads_local=heads_local, scale=scale, pieces=pieces)
    out = pl.pallas_call(
        kernel,
        grid_spec=grid_spec,
        out_shape=jax.ShapeDtypeStruct((shard_tok, width), jnp.bfloat16),
        compiler_params=pltpu.CompilerParams(dimension_semantics=("arbitrary",)),
    )(
        slot_window.reshape(-1),
        block_counts.astype(jnp.int32),
        bias,
        q_heads,
        *k_window,
        *v_window,
    )
    return lax.all_to_all(out, "head", split_axis=0, concat_axis=1, tiled=True)


def solution(mesh):
    in_specs = (
        P(("blk", "head"), None),
        P(("blk", "head"), None),
        P(("blk", "head"), None),
        P("blk", None),
        P("blk"),
        P(),
    )
    out_specs = P(("blk", "head"), None)
    return jax.shard_map(body, mesh=mesh, in_specs=in_specs, out_specs=out_specs, check_vma=False)
```

```python
import jax
import jax.numpy as jnp
from jax import lax
from jax.experimental import pallas as pl
from jax.experimental.pallas import tpu as pltpu
from jax.sharding import PartitionSpec as P

H = 48
DH = 128
TILE = 128
REACH = 3
SLOTS = 8
TILE_COUNT = 8

PIECE_OF_OFFSET = ((4, 1, 5, 0, 3, 2, 6), (5, 1, 3, 0, 6, 2, 4))


def permute(block, axis, route):
    return lax.ppermute(block, axis, route)


def shift_pairs(n, distance):
    return [(i, (i + distance) % n) for i in range(n)]


def attention_kernel(sw_ref, cnt_ref, bias_ref, q_ref, *refs, heads_local, scale, pieces):
    k_hbm = refs[:pieces]
    v_hbm = refs[pieces:2 * pieces]
    o_ref, k_buf, v_buf, sem = refs[2 * pieces:]
    i = pl.program_id(0)
    steps = pl.num_programs(0)
    parity = i % 2

    def copies(step, slot, c, p, j):
        k_copy = pltpu.make_async_copy(
            k_hbm[p].at[:, pl.ds(j * TILE, TILE)], k_buf.at[slot, :, pl.ds(c * TILE, TILE)], sem.at[0, slot, c]
        )
        v_copy = pltpu.make_async_copy(
            v_hbm[p].at[pl.ds(j * TILE, TILE), :], v_buf.at[slot, pl.ds(c * TILE, TILE), :], sem.at[1, slot, c]
        )
        return k_copy, v_copy

    def start(step, slot):
        for c in range(SLOTS):
            code = sw_ref[step * SLOTS + c]
            p_code = code // TILE_COUNT
            j = code % TILE_COUNT
            for p in range(pieces):
                @pl.when(jnp.logical_and(p_code == p, c < cnt_ref[step]))
                def _():
                    for copy in copies(step, slot, c, p, j):
                        copy.start()

    @pl.when(i == 0)
    def _():
        v_buf[...] = jnp.zeros(v_buf.shape, v_buf.dtype)
        start(0, 0)

    @pl.when(i + 1 < steps)
    def _():
        start(i + 1, 1 - parity)

    for c in range(SLOTS):
        @pl.when(c < cnt_ref[i])
        def _():
            for copy in copies(i, parity, c, 0, 0):
                copy.wait()

    count = cnt_ref[i]
    keys = SLOTS * TILE
    valid = lax.broadcasted_iota(jnp.int32, (TILE, keys), 1) < count * TILE
    k_all = k_buf.at[parity]
    v_all = v_buf.at[parity]
    for h in range(heads_local):
        cols = slice(h * DH, (h + 1) * DH)
        s = jnp.dot(q_ref[:, cols], k_all[cols, :], preferred_element_type=jnp.float32)
        s = s * scale
        s = s - bias_ref[h : h + 1, :]
        s = jnp.where(valid, s, -1e30)
        top = s.max(axis=1, keepdims=True)
        w = jnp.exp(s - top).astype(jnp.bfloat16)
        total = w.astype(jnp.float32).sum(axis=1, keepdims=True)
        acc = jnp.dot(w, v_all[:, cols], preferred_element_type=jnp.float32)
        o_ref[:, cols] = (acc / total).astype(o_ref.dtype)


def step_a(local, n):
    swap = [(i, i ^ 1) for i in range(n)]
    from_left2 = permute(local, "blk", shift_pairs(n, 2))
    from_right2 = permute(local, "blk", shift_pairs(n, -2))
    other_core = permute(local, "blk", swap)
    return from_left2, from_right2, other_core


def step_b(from_left2, from_right2, n):
    swap = [(i, i ^ 1) for i in range(n)]
    core = lax.axis_index("blk") % 2
    forward = jnp.where(core == 1, from_left2, from_right2)
    cross_route = [((i, (i + 1) % n) if i % 2 == 1 else (i, (i - 1) % n)) for i in range(n)]
    across = permute(forward, "blk", cross_route)
    other_left2 = permute(from_left2, "blk", swap)
    other_right2 = permute(from_right2, "blk", swap)
    return across, other_left2, other_right2


def body(queries, key_states, value_states, block_lists, block_counts, tile_order):
    cycle_size = lax.axis_size("blk")
    group_size = lax.axis_size("head")
    heads_local = H // group_size
    k_heads = lax.all_to_all(key_states, "head", split_axis=1, concat_axis=0, tiled=True)
    k_local = k_heads.T
    k_left2, k_right2, k_core = step_a(k_local, cycle_size)
    v_heads = lax.all_to_all(value_states, "head", split_axis=1, concat_axis=0, tiled=True)
    v_heads, k_left2, k_right2 = lax.optimization_barrier((v_heads, k_left2, k_right2))
    k_window = [k_local, k_left2, k_right2, k_core, *step_b(k_left2, k_right2, cycle_size)]
    v_left2, v_right2, v_core = step_a(v_heads, cycle_size)
    v_window = [v_heads, v_left2, v_right2, v_core, *step_b(v_left2, v_right2, cycle_size)]
    q_heads = lax.all_to_all(queries, "head", split_axis=1, concat_axis=0, tiled=True)
    shard_tok = q_heads.shape[0]
    tile_count = shard_tok // TILE
    width = heads_local * DH

    blk_index = lax.axis_index("blk")
    core = blk_index % 2
    shard_of = block_lists // tile_count
    offset = (shard_of - blk_index + REACH) % cycle_size
    table = jnp.array(PIECE_OF_OFFSET, dtype=jnp.int32)[core]
    slot_window = (table[offset] * tile_count + block_lists % tile_count).astype(jnp.int32)
    query_tile = blk_index * tile_count + jnp.arange(tile_count, dtype=jnp.int32)
    distance = (
        jnp.abs(tile_order[query_tile][:, None] - tile_order[block_lists]).astype(jnp.float32)
        / tile_order.shape[0]
    )
    head_index = lax.axis_index("head") * heads_local + jnp.arange(heads_local, dtype=jnp.int32)
    slopes = 8.0 * jnp.power(2.0, -8.0 * head_index.astype(jnp.float32) / H)
    bias = slopes[None, :, None, None] * distance[:, None, :, None]
    bias = jnp.broadcast_to(bias, (tile_count, heads_local, SLOTS, TILE)).reshape(tile_count, heads_local, SLOTS * TILE)
    scale = DH ** (-0.5)

    assert tile_count == TILE_COUNT
    pieces = len(k_window)
    any_spec = pl.BlockSpec(memory_space=pl.ANY)
    in_specs = (
        [
            pl.BlockSpec((None, heads_local, SLOTS * TILE), lambda i, sw, cnt: (i, 0, 0)),
            pl.BlockSpec((TILE, width), lambda i, sw, cnt: (i, 0)),
        ]
        + [any_spec] * (2 * pieces)
    )
    grid_spec = pltpu.PrefetchScalarGridSpec(
        num_scalar_prefetch=2,
        grid=(tile_count,),
        in_specs=in_specs,
        out_specs=pl.BlockSpec((TILE, width), lambda i, sw, cnt: (i, 0)),
        scratch_shapes=[
            pltpu.VMEM((2, width, SLOTS * TILE), jnp.bfloat16),
            pltpu.VMEM((2, SLOTS * TILE, width), jnp.bfloat16),
            pltpu.SemaphoreType.DMA((2, 2, SLOTS)),
        ],
    )
    kernel = lambda *args: attention_kernel(*args, heads_local=heads_local, scale=scale, pieces=pieces)
    out = pl.pallas_call(
        kernel,
        grid_spec=grid_spec,
        out_shape=jax.ShapeDtypeStruct((shard_tok, width), jnp.bfloat16),
        compiler_params=pltpu.CompilerParams(dimension_semantics=("arbitrary",)),
    )(
        slot_window.reshape(-1),
        block_counts.astype(jnp.int32),
        bias,
        q_heads,
        *k_window,
        *v_window,
    )
    return lax.all_to_all(out, "head", split_axis=0, concat_axis=1, tiled=True)


def solution(mesh):
    in_specs = (
        P(("blk", "head"), None),
        P(("blk", "head"), None),
        P(("blk", "head"), None),
        P("blk", None),
        P("blk"),
        P(),
    )
    out_specs = P(("blk", "head"), None)
    return jax.shard_map(body, mesh=mesh, in_specs=in_specs, out_specs=out_specs, check_vma=False)
```

```python
import jax
import jax.numpy as jnp
from jax import lax
from jax.experimental import pallas as pl
from jax.experimental.pallas import tpu as pltpu
from jax.sharding import PartitionSpec as P

H = 48
DH = 128
TILE = 128
REACH = 3
SLOTS = 8
TILE_COUNT = 8

PIECE_OF_OFFSET = ((4, 1, 5, 0, 3, 2, 6), (5, 1, 3, 0, 6, 2, 4))


def permute(block, axis, route):
    return lax.ppermute(block, axis, route)


def shift_pairs(n, distance):
    return [(i, (i + distance) % n) for i in range(n)]


def attention_kernel(sw_ref, cnt_ref, bias_ref, q_ref, *refs, heads_local, scale, pieces):
    k_hbm = refs[:pieces]
    v_hbm = refs[pieces:2 * pieces]
    o_ref, k_buf, v_buf, sem, s_buf = refs[2 * pieces:]
    i = pl.program_id(0)
    steps = pl.num_programs(0)
    parity = i % 2

    def copies(step, slot, c, p, j):
        k_copy = pltpu.make_async_copy(
            k_hbm[p].at[:, pl.ds(j * TILE, TILE)], k_buf.at[slot, :, pl.ds(c * TILE, TILE)], sem.at[0, slot, c]
        )
        v_copy = pltpu.make_async_copy(
            v_hbm[p].at[pl.ds(j * TILE, TILE), :], v_buf.at[slot, pl.ds(c * TILE, TILE), :], sem.at[1, slot, c]
        )
        return k_copy, v_copy

    def start(step, slot):
        for c in range(SLOTS):
            code = sw_ref[step * SLOTS + c]
            p_code = code // TILE_COUNT
            j = code % TILE_COUNT
            for p in range(pieces):
                @pl.when(jnp.logical_and(p_code == p, c < cnt_ref[step]))
                def _():
                    for copy in copies(step, slot, c, p, j):
                        copy.start()

    @pl.when(i == 0)
    def _():
        start(0, 0)

    @pl.when(i + 1 < steps)
    def _():
        start(i + 1, 1 - parity)

    for c in range(SLOTS):
        @pl.when(c < cnt_ref[i])
        def _():
            for copy in copies(i, parity, c, 0, 0):
                copy.wait()

    count = cnt_ref[i]
    k_all = k_buf.at[parity]
    v_all = v_buf.at[parity]
    for h in range(heads_local):
        cols = slice(h * DH, (h + 1) * DH)
        q = q_ref[:, cols]

        def score_pass(c, top):
            keys = pl.ds(pl.multiple_of(c * TILE, TILE), TILE)
            s = jnp.dot(q, k_all[cols, keys], preferred_element_type=jnp.float32)
            s = s * scale
            s = s - bias_ref[h : h + 1, keys]
            s_buf[c] = s
            return jnp.maximum(top, s.max(axis=1, keepdims=True))

        top = lax.fori_loop(0, count, score_pass, jnp.full((TILE, 1), -jnp.inf, jnp.float32))

        def weight_pass(c, carry):
            total, acc = carry
            keys = pl.ds(pl.multiple_of(c * TILE, TILE), TILE)
            w = jnp.exp(s_buf[c] - top).astype(jnp.bfloat16)
            total = total + w.astype(jnp.float32).sum(axis=1, keepdims=True)
            acc = acc + jnp.dot(w, v_all[keys, cols], preferred_element_type=jnp.float32)
            return total, acc

        zero = (jnp.zeros((TILE, 1), jnp.float32), jnp.zeros((TILE, DH), jnp.float32))
        total, acc = lax.fori_loop(0, count, weight_pass, zero)
        o_ref[:, cols] = (acc / total).astype(o_ref.dtype)


def exchange(local, axis, n):
    swap = [(i, i ^ 1) for i in range(n)]
    from_left2 = permute(local, "blk", shift_pairs(n, 2))
    from_right2 = permute(local, "blk", shift_pairs(n, -2))
    other_core = permute(local, "blk", swap)
    core = lax.axis_index("blk") % 2
    forward = jnp.where(core == 1, from_left2, from_right2)
    cross_route = [((i, (i + 1) % n) if i % 2 == 1 else (i, (i - 1) % n)) for i in range(n)]
    across = permute(forward, "blk", cross_route)
    other_left2 = permute(from_left2, "blk", swap)
    other_right2 = permute(from_right2, "blk", swap)
    return [local, from_left2, from_right2, other_core, across, other_left2, other_right2]


def body(queries, key_states, value_states, block_lists, block_counts, tile_order):
    cycle_size = lax.axis_size("blk")
    group_size = lax.axis_size("head")
    heads_local = H // group_size
    k_heads = lax.all_to_all(key_states, "head", split_axis=1, concat_axis=0, tiled=True)
    k_window = exchange(k_heads.T, 1, cycle_size)
    v_heads = lax.all_to_all(value_states, "head", split_axis=1, concat_axis=0, tiled=True)
    v_window = exchange(v_heads, 0, cycle_size)
    q_heads = lax.all_to_all(queries, "head", split_axis=1, concat_axis=0, tiled=True)
    shard_tok = q_heads.shape[0]
    tile_count = shard_tok // TILE
    width = heads_local * DH

    blk_index = lax.axis_index("blk")
    core = blk_index % 2
    shard_of = block_lists // tile_count
    offset = (shard_of - blk_index + REACH) % cycle_size
    table = jnp.array(PIECE_OF_OFFSET, dtype=jnp.int32)[core]
    slot_window = (table[offset] * tile_count + block_lists % tile_count).astype(jnp.int32)
    query_tile = blk_index * tile_count + jnp.arange(tile_count, dtype=jnp.int32)
    distance = (
        jnp.abs(tile_order[query_tile][:, None] - tile_order[block_lists]).astype(jnp.float32)
        / tile_order.shape[0]
    )
    head_index = lax.axis_index("head") * heads_local + jnp.arange(heads_local, dtype=jnp.int32)
    slopes = 8.0 * jnp.power(2.0, -8.0 * head_index.astype(jnp.float32) / H)
    bias = slopes[None, :, None, None] * distance[:, None, :, None]
    bias = jnp.broadcast_to(bias, (tile_count, heads_local, SLOTS, TILE)).reshape(tile_count, heads_local, SLOTS * TILE)
    scale = DH ** (-0.5)

    assert tile_count == TILE_COUNT
    pieces = len(k_window)
    any_spec = pl.BlockSpec(memory_space=pl.ANY)
    in_specs = (
        [
            pl.BlockSpec((None, heads_local, SLOTS * TILE), lambda i, sw, cnt: (i, 0, 0)),
            pl.BlockSpec((TILE, width), lambda i, sw, cnt: (i, 0)),
        ]
        + [any_spec] * (2 * pieces)
    )
    grid_spec = pltpu.PrefetchScalarGridSpec(
        num_scalar_prefetch=2,
        grid=(tile_count,),
        in_specs=in_specs,
        out_specs=pl.BlockSpec((TILE, width), lambda i, sw, cnt: (i, 0)),
        scratch_shapes=[
            pltpu.VMEM((2, width, SLOTS * TILE), jnp.bfloat16),
            pltpu.VMEM((2, SLOTS * TILE, width), jnp.bfloat16),
            pltpu.SemaphoreType.DMA((2, 2, SLOTS)),
            pltpu.VMEM((SLOTS, TILE, TILE), jnp.float32),
        ],
    )
    kernel = lambda *args: attention_kernel(*args, heads_local=heads_local, scale=scale, pieces=pieces)
    out = pl.pallas_call(
        kernel,
        grid_spec=grid_spec,
        out_shape=jax.ShapeDtypeStruct((shard_tok, width), jnp.bfloat16),
        compiler_params=pltpu.CompilerParams(dimension_semantics=("arbitrary",)),
    )(
        slot_window.reshape(-1),
        block_counts.astype(jnp.int32),
        bias,
        q_heads,
        *k_window,
        *v_window,
    )
    return lax.all_to_all(out, "head", split_axis=0, concat_axis=1, tiled=True)


def solution(mesh):
    in_specs = (
        P(("blk", "head"), None),
        P(("blk", "head"), None),
        P(("blk", "head"), None),
        P("blk", None),
        P("blk"),
        P(),
    )
    out_specs = P(("blk", "head"), None)
    return jax.shard_map(body, mesh=mesh, in_specs=in_specs, out_specs=out_specs, check_vma=False)
```

```python
import jax
import jax.numpy as jnp
from jax import lax
from jax.experimental import pallas as pl
from jax.experimental.pallas import tpu as pltpu
from jax.sharding import PartitionSpec as P

H = 48
DH = 128
TILE = 128
REACH = 3
SLOTS = 8
TILE_COUNT = 8

PIECE_OF_OFFSET = ((4, 1, 5, 0, 3, 2, 6), (5, 1, 3, 0, 6, 2, 4))


def permute(block, axis, route):
    return lax.ppermute(block, axis, route)


def shift_pairs(n, distance):
    return [(i, (i + distance) % n) for i in range(n)]


def attention_kernel(sw_ref, cnt_ref, bias_ref, q_ref, *refs, heads_local, scale, pieces, rows):
    k_hbm = refs[:pieces]
    v_hbm = refs[pieces:2 * pieces]
    o_ref, k_buf, v_buf, sem = refs[2 * pieces:]
    i = pl.program_id(0)
    steps = pl.num_programs(0)
    parity = i % 2

    def copies(step, slot, c, p, j):
        k_copy = pltpu.make_async_copy(
            k_hbm[p].at[:, pl.ds(j * TILE, TILE)], k_buf.at[slot, :, pl.ds(c * TILE, TILE)], sem.at[0, slot, c]
        )
        v_copy = pltpu.make_async_copy(
            v_hbm[p].at[pl.ds(j * TILE, TILE), :], v_buf.at[slot, pl.ds(c * TILE, TILE), :], sem.at[1, slot, c]
        )
        return k_copy, v_copy

    def start(step, slot):
        for c in range(SLOTS):
            code = sw_ref[step * SLOTS + c]
            p_code = code // TILE_COUNT
            j = code % TILE_COUNT
            for p in range(pieces):
                @pl.when(jnp.logical_and(p_code == p, c < cnt_ref[step]))
                def _():
                    for copy in copies(step, slot, c, p, j):
                        copy.start()

    @pl.when(i == 0)
    def _():
        v_buf[...] = jnp.zeros(v_buf.shape, v_buf.dtype)
        start(0, 0)

    @pl.when(i + 1 < steps)
    def _():
        start(i + 1, 1 - parity)

    for c in range(SLOTS):
        @pl.when(c < cnt_ref[i])
        def _():
            for copy in copies(i, parity, c, 0, 0):
                copy.wait()

    count = cnt_ref[i]
    keys = SLOTS * TILE
    valid = lax.broadcasted_iota(jnp.int32, (rows, keys), 1) < count * TILE
    k_all = k_buf.at[parity]
    v_all = v_buf.at[parity]
    for h in range(heads_local):
        cols = slice(h * DH, (h + 1) * DH)
        s = jnp.dot(q_ref[:, cols], k_all[cols, :], preferred_element_type=jnp.float32)
        s = s * scale
        s = s - bias_ref[h : h + 1, :]
        s = jnp.where(valid, s, -1e30)
        top = s.max(axis=1, keepdims=True)
        w = jnp.exp(s - top).astype(jnp.bfloat16)
        total = w.astype(jnp.float32).sum(axis=1, keepdims=True)
        acc = jnp.dot(w, v_all[:, cols], preferred_element_type=jnp.float32)
        o_ref[:, cols] = (acc / total).astype(o_ref.dtype)


def exchange(local, axis, n):
    swap = [(i, i ^ 1) for i in range(n)]
    from_left2 = permute(local, "blk", shift_pairs(n, 2))
    from_right2 = permute(local, "blk", shift_pairs(n, -2))
    other_core = permute(local, "blk", swap)
    core = lax.axis_index("blk") % 2
    forward = jnp.where(core == 1, from_left2, from_right2)
    cross_route = [((i, (i + 1) % n) if i % 2 == 1 else (i, (i - 1) % n)) for i in range(n)]
    across = permute(forward, "blk", cross_route)
    other_left2 = permute(from_left2, "blk", swap)
    other_right2 = permute(from_right2, "blk", swap)
    return [local, from_left2, from_right2, other_core, across, other_left2, other_right2]


def body(queries, key_states, value_states, block_lists, block_counts, tile_order):
    cycle_size = lax.axis_size("blk")
    group_size = lax.axis_size("head")
    heads_local = H // group_size
    k_heads = lax.all_to_all(key_states, "head", split_axis=1, concat_axis=0, tiled=True)
    k_window = exchange(k_heads.T, 1, cycle_size)
    v_heads = lax.all_to_all(value_states, "head", split_axis=1, concat_axis=0, tiled=True)
    v_window = exchange(v_heads, 0, cycle_size)
    q_heads = lax.all_to_all(queries, "head", split_axis=1, concat_axis=0, tiled=True)
    shard_tok = q_heads.shape[0]
    tile_count = shard_tok // TILE
    width = heads_local * DH

    blk_index = lax.axis_index("blk")
    core = blk_index % 2
    shard_of = block_lists // tile_count
    offset = (shard_of - blk_index + REACH) % cycle_size
    table = jnp.array(PIECE_OF_OFFSET, dtype=jnp.int32)[core]
    slot_window = (table[offset] * tile_count + block_lists % tile_count).astype(jnp.int32)
    query_tile = blk_index * tile_count + jnp.arange(tile_count, dtype=jnp.int32)
    distance = (
        jnp.abs(tile_order[query_tile][:, None] - tile_order[block_lists]).astype(jnp.float32)
        / tile_order.shape[0]
    )
    head_index = lax.axis_index("head") * heads_local + jnp.arange(heads_local, dtype=jnp.int32)
    slopes = 8.0 * jnp.power(2.0, -8.0 * head_index.astype(jnp.float32) / H)
    bias = slopes[None, :, None, None] * distance[:, None, :, None]
    bias = jnp.broadcast_to(bias, (tile_count, heads_local, SLOTS, TILE)).reshape(tile_count, heads_local, SLOTS * TILE)
    scale = DH ** (-0.5)

    assert tile_count == TILE_COUNT
    pieces = len(k_window)
    rows = TILE // 2
    any_spec = pl.BlockSpec(memory_space=pl.ANY)

    def half_call(half):
        in_specs = (
            [
                pl.BlockSpec((None, heads_local, SLOTS * TILE), lambda i, sw, cnt: (i, 0, 0)),
                pl.BlockSpec((rows, width), lambda i, sw, cnt: (2 * i + half, 0)),
            ]
            + [any_spec] * (2 * pieces)
        )
        grid_spec = pltpu.PrefetchScalarGridSpec(
            num_scalar_prefetch=2,
            grid=(tile_count,),
            in_specs=in_specs,
            out_specs=pl.BlockSpec((rows, width), lambda i, sw, cnt: (i, 0)),
            scratch_shapes=[
                pltpu.VMEM((2, width, SLOTS * TILE), jnp.bfloat16),
                pltpu.VMEM((2, SLOTS * TILE, width), jnp.bfloat16),
                pltpu.SemaphoreType.DMA((2, 2, SLOTS)),
            ],
        )
        kernel = lambda *args: attention_kernel(
            *args, heads_local=heads_local, scale=scale, pieces=pieces, rows=rows
        )
        out = pl.pallas_call(
            kernel,
            grid_spec=grid_spec,
            out_shape=jax.ShapeDtypeStruct((tile_count * rows, width), jnp.bfloat16),
            compiler_params=pltpu.CompilerParams(dimension_semantics=("arbitrary",)),
        )(
            slot_window.reshape(-1),
            block_counts.astype(jnp.int32),
            bias,
            q_heads,
            *k_window,
            *v_window,
        )
        return lax.all_to_all(out, "head", split_axis=0, concat_axis=1, tiled=True)

    return jnp.concatenate([half_call(0), half_call(1)], axis=0)


def solution(mesh):
    in_specs = (
        P(("blk", "head"), None),
        P(("blk", "head"), None),
        P(("blk", "head"), None),
        P("blk", None),
        P("blk"),
        P(),
    )
    out_specs = P(("blk", "head"), None)
    return jax.shard_map(body, mesh=mesh, in_specs=in_specs, out_specs=out_specs, check_vma=False)
```

```python
import jax
import jax.numpy as jnp
from jax import lax
from jax.experimental import pallas as pl
from jax.experimental.pallas import tpu as pltpu
from jax.sharding import PartitionSpec as P

H = 48
DH = 128
TILE = 128
REACH = 3
SLOTS = 8
TILE_COUNT = 8

PIECE_OF_OFFSET = ((4, 1, 6, 0, 3, 2, 7), (6, 1, 3, 0, 7, 2, 5))


def permute(block, axis, route):
    return lax.ppermute(block, axis, route)


def shift_pairs(n, distance):
    return [(i, (i + distance) % n) for i in range(n)]


def attention_kernel(sw_ref, cnt_ref, bias_ref, q_ref, *refs, heads_local, scale, pieces):
    k_hbm = refs[:pieces]
    v_hbm = refs[pieces:2 * pieces]
    o_ref, k_buf, v_buf, sem = refs[2 * pieces:]
    i = pl.program_id(0)
    steps = pl.num_programs(0)
    parity = i % 2

    def copies(step, slot, c, p, j):
        k_copy = pltpu.make_async_copy(
            k_hbm[p].at[:, pl.ds(j * TILE, TILE)], k_buf.at[slot, :, pl.ds(c * TILE, TILE)], sem.at[0, slot, c]
        )
        v_copy = pltpu.make_async_copy(
            v_hbm[p].at[pl.ds(j * TILE, TILE), :], v_buf.at[slot, pl.ds(c * TILE, TILE), :], sem.at[1, slot, c]
        )
        return k_copy, v_copy

    def start(step, slot):
        for c in range(SLOTS):
            code = sw_ref[step * SLOTS + c]
            p_code = code // TILE_COUNT
            j = code % TILE_COUNT
            for p in range(pieces):
                @pl.when(jnp.logical_and(p_code == p, c < cnt_ref[step]))
                def _():
                    for copy in copies(step, slot, c, p, j):
                        copy.start()

    @pl.when(i == 0)
    def _():
        v_buf[...] = jnp.zeros(v_buf.shape, v_buf.dtype)
        start(0, 0)

    @pl.when(i + 1 < steps)
    def _():
        start(i + 1, 1 - parity)

    for c in range(SLOTS):
        @pl.when(c < cnt_ref[i])
        def _():
            for copy in copies(i, parity, c, 0, 0):
                copy.wait()

    count = cnt_ref[i]
    keys = SLOTS * TILE
    valid = lax.broadcasted_iota(jnp.int32, (TILE, keys), 1) < count * TILE
    k_all = k_buf.at[parity]
    v_all = v_buf.at[parity]
    for h in range(heads_local):
        cols = slice(h * DH, (h + 1) * DH)
        s = jnp.dot(q_ref[:, cols], k_all[cols, :], preferred_element_type=jnp.float32)
        s = s * scale
        s = s - bias_ref[h : h + 1, :]
        s = jnp.where(valid, s, -1e30)
        top = s.max(axis=1, keepdims=True)
        w = jnp.exp(s - top).astype(jnp.bfloat16)
        total = w.astype(jnp.float32).sum(axis=1, keepdims=True)
        acc = jnp.dot(w, v_all[:, cols], preferred_element_type=jnp.float32)
        o_ref[:, cols] = (acc / total).astype(o_ref.dtype)


def exchange(local, axis, n):
    swap = [(i, i ^ 1) for i in range(n)]
    from_left2 = permute(local, "blk", shift_pairs(n, 2))
    from_right2 = permute(local, "blk", shift_pairs(n, -2))
    other_core = permute(local, "blk", swap)
    odd_ahead = permute(from_left2, "blk", [(i, (i + 1) % n) for i in range(1, n, 2)])
    even_back = permute(from_right2, "blk", [(i, (i - 1) % n) for i in range(0, n, 2)])
    other_left2 = permute(from_left2, "blk", swap)
    other_right2 = permute(from_right2, "blk", swap)
    return [local, from_left2, from_right2, other_core, odd_ahead, even_back, other_left2, other_right2]


def body(queries, key_states, value_states, block_lists, block_counts, tile_order):
    cycle_size = lax.axis_size("blk")
    group_size = lax.axis_size("head")
    heads_local = H // group_size
    q_and_k = jnp.stack((queries, key_states))
    q_heads, k_heads = lax.all_to_all(q_and_k, "head", split_axis=2, concat_axis=1, tiled=True)
    k_window = exchange(k_heads.T, 1, cycle_size)
    v_heads = lax.all_to_all(value_states, "head", split_axis=1, concat_axis=0, tiled=True)
    v_window = exchange(v_heads, 0, cycle_size)
    shard_tok = q_heads.shape[0]
    tile_count = shard_tok // TILE
    width = heads_local * DH

    blk_index = lax.axis_index("blk")
    core = blk_index % 2
    shard_of = block_lists // tile_count
    offset = (shard_of - blk_index + REACH) % cycle_size
    table = jnp.array(PIECE_OF_OFFSET, dtype=jnp.int32)[core]
    slot_window = (table[offset] * tile_count + block_lists % tile_count).astype(jnp.int32)
    query_tile = blk_index * tile_count + jnp.arange(tile_count, dtype=jnp.int32)
    distance = (
        jnp.abs(tile_order[query_tile][:, None] - tile_order[block_lists]).astype(jnp.float32)
        / tile_order.shape[0]
    )
    head_index = lax.axis_index("head") * heads_local + jnp.arange(heads_local, dtype=jnp.int32)
    slopes = 8.0 * jnp.power(2.0, -8.0 * head_index.astype(jnp.float32) / H)
    bias = slopes[None, :, None, None] * distance[:, None, :, None]
    bias = jnp.broadcast_to(bias, (tile_count, heads_local, SLOTS, TILE)).reshape(tile_count, heads_local, SLOTS * TILE)
    scale = DH ** (-0.5)

    assert tile_count == TILE_COUNT
    pieces = len(k_window)
    any_spec = pl.BlockSpec(memory_space=pl.ANY)
    in_specs = (
        [
            pl.BlockSpec((None, heads_local, SLOTS * TILE), lambda i, sw, cnt: (i, 0, 0)),
            pl.BlockSpec((TILE, width), lambda i, sw, cnt: (i, 0)),
        ]
        + [any_spec] * (2 * pieces)
    )
    grid_spec = pltpu.PrefetchScalarGridSpec(
        num_scalar_prefetch=2,
        grid=(tile_count,),
        in_specs=in_specs,
        out_specs=pl.BlockSpec((TILE, width), lambda i, sw, cnt: (i, 0)),
        scratch_shapes=[
            pltpu.VMEM((2, width, SLOTS * TILE), jnp.bfloat16),
            pltpu.VMEM((2, SLOTS * TILE, width), jnp.bfloat16),
            pltpu.SemaphoreType.DMA((2, 2, SLOTS)),
        ],
    )
    kernel = lambda *args: attention_kernel(*args, heads_local=heads_local, scale=scale, pieces=pieces)
    out = pl.pallas_call(
        kernel,
        grid_spec=grid_spec,
        out_shape=jax.ShapeDtypeStruct((shard_tok, width), jnp.bfloat16),
        compiler_params=pltpu.CompilerParams(dimension_semantics=("arbitrary",)),
    )(
        slot_window.reshape(-1),
        block_counts.astype(jnp.int32),
        bias,
        q_heads,
        *k_window,
        *v_window,
    )
    return lax.all_to_all(out, "head", split_axis=0, concat_axis=1, tiled=True)


def solution(mesh):
    in_specs = (
        P(("blk", "head"), None),
        P(("blk", "head"), None),
        P(("blk", "head"), None),
        P("blk", None),
        P("blk"),
        P(),
    )
    out_specs = P(("blk", "head"), None)
    return jax.shard_map(body, mesh=mesh, in_specs=in_specs, out_specs=out_specs, check_vma=False)
```

```python
import jax
import jax.numpy as jnp
from jax import lax
from jax.experimental import pallas as pl
from jax.experimental.pallas import tpu as pltpu
from jax.sharding import PartitionSpec as P

H = 48
DH = 128
TILE = 128
REACH = 3
SLOTS = 8
TILE_COUNT = 8

PIECE_OF_OFFSET = ((4, 1, 5, 0, 3, 2, 6), (5, 1, 3, 0, 6, 2, 4))


def permute(block, axis, route):
    return lax.ppermute(block, axis, route)


def shift_pairs(n, distance):
    return [(i, (i + distance) % n) for i in range(n)]


def attention_kernel(sw_ref, cnt_ref, bias_ref, q_ref, *refs, heads_local, scale, pieces):
    k_hbm = refs[:pieces]
    v_hbm = refs[pieces:2 * pieces]
    o_ref, k_buf, v_buf, sem = refs[2 * pieces:]
    i = pl.program_id(0)
    steps = pl.num_programs(0)
    parity = i % 2

    def copies(slot, c, p, j):
        k_copy = pltpu.make_async_copy(
            k_hbm[p].at[pl.ds(j * TILE, TILE), :], k_buf.at[slot, pl.ds(c * TILE, TILE), :], sem.at[0, slot, c]
        )
        v_copy = pltpu.make_async_copy(
            v_hbm[p].at[:, pl.ds(j * TILE, TILE)], v_buf.at[slot, :, pl.ds(c * TILE, TILE)], sem.at[1, slot, c]
        )
        return k_copy, v_copy

    def start(step, slot):
        for c in range(SLOTS):
            code = sw_ref[step * SLOTS + c]
            p_code = code // TILE_COUNT
            j = code % TILE_COUNT
            for p in range(pieces):
                @pl.when(p_code == p)
                def _():
                    for copy in copies(slot, c, p, j):
                        copy.start()

    @pl.when(i == 0)
    def _():
        start(0, 0)

    @pl.when(i + 1 < steps)
    def _():
        start(i + 1, 1 - parity)

    for c in range(SLOTS):
        for copy in copies(parity, c, 0, 0):
            copy.wait()

    count = cnt_ref[i]
    keys = SLOTS * TILE
    valid = lax.broadcasted_iota(jnp.int32, (keys, TILE), 0) < count * TILE
    k_all = k_buf.at[parity]
    v_all = v_buf.at[parity]
    for h in range(heads_local):
        cols = slice(h * DH, (h + 1) * DH)
        s = jnp.dot(k_all[:, cols], q_ref[cols, :], preferred_element_type=jnp.float32)
        s = s * scale
        s = s - bias_ref[h]
        s = jnp.where(valid, s, -1e30)
        top = s.max(axis=0, keepdims=True)
        w = jnp.exp(s - top).astype(jnp.bfloat16)
        total = w.astype(jnp.float32).sum(axis=0, keepdims=True)
        acc = jnp.dot(v_all[cols, :], w, preferred_element_type=jnp.float32)
        o_ref[cols, :] = (acc / total).astype(o_ref.dtype)


def exchange(local, axis, n):
    swap = [(i, i ^ 1) for i in range(n)]
    from_left2 = permute(local, "blk", shift_pairs(n, 2))
    from_right2 = permute(local, "blk", shift_pairs(n, -2))
    other_core = permute(local, "blk", swap)
    core = lax.axis_index("blk") % 2
    forward = jnp.where(core == 1, from_left2, from_right2)
    cross_route = [((i, (i + 1) % n) if i % 2 == 1 else (i, (i - 1) % n)) for i in range(n)]
    across = permute(forward, "blk", cross_route)
    other_left2 = permute(from_left2, "blk", swap)
    other_right2 = permute(from_right2, "blk", swap)
    return [local, from_left2, from_right2, other_core, across, other_left2, other_right2]


def body(queries, key_states, value_states, block_lists, block_counts, tile_order):
    cycle_size = lax.axis_size("blk")
    group_size = lax.axis_size("head")
    heads_local = H // group_size
    k_heads = lax.all_to_all(key_states, "head", split_axis=1, concat_axis=0, tiled=True)
    k_window = exchange(k_heads, 0, cycle_size)
    v_heads = lax.all_to_all(value_states, "head", split_axis=1, concat_axis=0, tiled=True)
    v_window = exchange(v_heads.T, 1, cycle_size)
    q_heads = lax.all_to_all(queries, "head", split_axis=1, concat_axis=0, tiled=True)
    shard_tok = q_heads.shape[0]
    tile_count = shard_tok // TILE
    width = heads_local * DH

    blk_index = lax.axis_index("blk")
    core = blk_index % 2
    shard_of = block_lists // tile_count
    offset = (shard_of - blk_index + REACH) % cycle_size
    table = jnp.array(PIECE_OF_OFFSET, dtype=jnp.int32)[core]
    slot_window = (table[offset] * tile_count + block_lists % tile_count).astype(jnp.int32)
    query_tile = blk_index * tile_count + jnp.arange(tile_count, dtype=jnp.int32)
    distance = (
        jnp.abs(tile_order[query_tile][:, None] - tile_order[block_lists]).astype(jnp.float32)
        / tile_order.shape[0]
    )
    head_index = lax.axis_index("head") * heads_local + jnp.arange(heads_local, dtype=jnp.int32)
    slopes = 8.0 * jnp.power(2.0, -8.0 * head_index.astype(jnp.float32) / H)
    bias = slopes[None, :, None, None] * distance[:, None, :, None]
    bias = jnp.broadcast_to(bias, (tile_count, heads_local, SLOTS, TILE)).reshape(tile_count, heads_local, SLOTS * TILE, 1)
    scale = DH ** (-0.5)

    assert tile_count == TILE_COUNT
    pieces = len(k_window)
    any_spec = pl.BlockSpec(memory_space=pl.ANY)
    in_specs = (
        [
            pl.BlockSpec((None, heads_local, SLOTS * TILE, 1), lambda i, sw, cnt: (i, 0, 0, 0)),
            pl.BlockSpec((width, TILE), lambda i, sw, cnt: (0, i)),
        ]
        + [any_spec] * (2 * pieces)
    )
    grid_spec = pltpu.PrefetchScalarGridSpec(
        num_scalar_prefetch=2,
        grid=(tile_count,),
        in_specs=in_specs,
        out_specs=pl.BlockSpec((width, TILE), lambda i, sw, cnt: (0, i)),
        scratch_shapes=[
            pltpu.VMEM((2, SLOTS * TILE, width), jnp.bfloat16),
            pltpu.VMEM((2, width, SLOTS * TILE), jnp.bfloat16),
            pltpu.SemaphoreType.DMA((2, 2, SLOTS)),
        ],
    )
    kernel = lambda *args: attention_kernel(*args, heads_local=heads_local, scale=scale, pieces=pieces)
    out = pl.pallas_call(
        kernel,
        grid_spec=grid_spec,
        out_shape=jax.ShapeDtypeStruct((width, shard_tok), jnp.bfloat16),
        compiler_params=pltpu.CompilerParams(dimension_semantics=("arbitrary",)),
    )(
        slot_window.reshape(-1),
        block_counts.astype(jnp.int32),
        bias,
        q_heads.T,
        *k_window,
        *v_window,
    )
    return lax.all_to_all(out.T, "head", split_axis=0, concat_axis=1, tiled=True)


def solution(mesh):
    in_specs = (
        P(("blk", "head"), None),
        P(("blk", "head"), None),
        P(("blk", "head"), None),
        P("blk", None),
        P("blk"),
        P(),
    )
    out_specs = P(("blk", "head"), None)
    return jax.shard_map(body, mesh=mesh, in_specs=in_specs, out_specs=out_specs, check_vma=False)
```

```python
import jax
import jax.numpy as jnp
from jax import lax
from jax.experimental import pallas as pl
from jax.experimental.pallas import tpu as pltpu
from jax.sharding import PartitionSpec as P

H = 48
DH = 128
TILE = 128
REACH = 3
SLOTS = 8
TILE_COUNT = 8

PIECE_OF_OFFSET = ((4, 1, 5, 0, 3, 2, 6), (5, 1, 3, 0, 6, 2, 4))


def permute(block, axis, route):
    return lax.ppermute(block, axis, route)


def shift_pairs(n, distance):
    return [(i, (i + distance) % n) for i in range(n)]


def attention_kernel(sw_ref, cnt_ref, bias_ref, q_ref, *refs, heads_local, scale, pieces):
    k_hbm = refs[:pieces]
    v_hbm = refs[pieces:2 * pieces]
    o_ref, k_buf, v_buf, sem = refs[2 * pieces:]
    i = pl.program_id(0)
    steps = pl.num_programs(0)
    parity = i % 2

    def copies(step, slot, c, p, j):
        k_copy = pltpu.make_async_copy(k_hbm[p].at[:, pl.ds(j * TILE, TILE)], k_buf.at[slot, c], sem.at[0, slot, c])
        v_copy = pltpu.make_async_copy(v_hbm[p].at[pl.ds(j * TILE, TILE), :], v_buf.at[slot, c], sem.at[1, slot, c])
        return k_copy, v_copy

    def start(step, slot):
        for c in range(SLOTS):
            code = sw_ref[step * SLOTS + c]
            p_code = code // TILE_COUNT
            j = code % TILE_COUNT
            for p in range(pieces):
                @pl.when(p_code == p)
                def _():
                    for copy in copies(step, slot, c, p, j):
                        copy.start()

    @pl.when(i == 0)
    def _():
        start(0, 0)

    @pl.when(i + 1 < steps)
    def _():
        start(i + 1, 1 - parity)

    for c in range(SLOTS):
        for copy in copies(i, parity, c, 0, 0):
            copy.wait()

    count = cnt_ref[i]
    for h in range(heads_local):
        cols = slice(h * DH, (h + 1) * DH)
        q = q_ref[:, cols]
        scores = []
        for c in range(SLOTS):
            s = jnp.dot(q, k_buf[parity, c, cols, :], preferred_element_type=jnp.float32)
            s = s * scale
            s = s - bias_ref[(i * SLOTS + c) * heads_local + h]
            s = jnp.where(c < count, s, -1e30)
            scores.append(s)
        top = scores[0].max(axis=1, keepdims=True)
        for c in range(1, SLOTS):
            top = jnp.maximum(top, scores[c].max(axis=1, keepdims=True))
        total = jnp.zeros((TILE, 1), jnp.float32)
        acc = jnp.zeros((TILE, DH), jnp.float32)
        for c in range(SLOTS):
            w = jnp.exp(scores[c] - top).astype(jnp.bfloat16)
            total = total + w.astype(jnp.float32).sum(axis=1, keepdims=True)
            acc = acc + jnp.dot(w, v_buf[parity, c, :, cols], preferred_element_type=jnp.float32)
        o_ref[:, cols] = (acc / total).astype(o_ref.dtype)


def exchange(local, axis, n):
    swap = [(i, i ^ 1) for i in range(n)]
    from_left2 = permute(local, "blk", shift_pairs(n, 2))
    from_right2 = permute(local, "blk", shift_pairs(n, -2))
    other_core = permute(local, "blk", swap)
    core = lax.axis_index("blk") % 2
    forward = jnp.where(core == 1, from_left2, from_right2)
    cross_route = [((i, (i + 1) % n) if i % 2 == 1 else (i, (i - 1) % n)) for i in range(n)]
    across = permute(forward, "blk", cross_route)
    other_left2 = permute(from_left2, "blk", swap)
    other_right2 = permute(from_right2, "blk", swap)
    return [local, from_left2, from_right2, other_core, across, other_left2, other_right2]


def body(queries, key_states, value_states, block_lists, block_counts, tile_order):
    cycle_size = lax.axis_size("blk")
    group_size = lax.axis_size("head")
    heads_local = H // group_size
    k_heads = lax.all_to_all(key_states, "head", split_axis=1, concat_axis=0, tiled=True)
    k_window = exchange(k_heads.T, 1, cycle_size)
    v_heads = lax.all_to_all(value_states, "head", split_axis=1, concat_axis=0, tiled=True)
    v_window = exchange(v_heads, 0, cycle_size)
    queries, k_window, v_window = lax.optimization_barrier((queries, k_window, v_window))
    q_heads = lax.all_to_all(queries, "head", split_axis=1, concat_axis=0, tiled=True)
    shard_tok = q_heads.shape[0]
    tile_count = shard_tok // TILE
    width = heads_local * DH

    blk_index = lax.axis_index("blk")
    core = blk_index % 2
    shard_of = block_lists // tile_count
    offset = (shard_of - blk_index + REACH) % cycle_size
    table = jnp.array(PIECE_OF_OFFSET, dtype=jnp.int32)[core]
    slot_window = (table[offset] * tile_count + block_lists % tile_count).astype(jnp.int32)
    query_tile = blk_index * tile_count + jnp.arange(tile_count, dtype=jnp.int32)
    distance = (
        jnp.abs(tile_order[query_tile][:, None] - tile_order[block_lists]).astype(jnp.float32)
        / tile_order.shape[0]
    )
    head_index = lax.axis_index("head") * heads_local + jnp.arange(heads_local, dtype=jnp.int32)
    slopes = 8.0 * jnp.power(2.0, -8.0 * head_index.astype(jnp.float32) / H)
    bias = (slopes[None, None, :] * distance[:, :, None]).reshape(-1)
    scale = DH ** (-0.5)

    assert tile_count == TILE_COUNT
    pieces = len(k_window)
    any_spec = pl.BlockSpec(memory_space=pl.ANY)
    in_specs = (
        [pl.BlockSpec(memory_space=pltpu.SMEM), pl.BlockSpec((TILE, width), lambda i, sw, cnt: (i, 0))]
        + [any_spec] * (2 * pieces)
    )
    grid_spec = pltpu.PrefetchScalarGridSpec(
        num_scalar_prefetch=2,
        grid=(tile_count,),
        in_specs=in_specs,
        out_specs=pl.BlockSpec((TILE, width), lambda i, sw, cnt: (i, 0)),
        scratch_shapes=[
            pltpu.VMEM((2, SLOTS, width, TILE), jnp.bfloat16),
            pltpu.VMEM((2, SLOTS, TILE, width), jnp.bfloat16),
            pltpu.SemaphoreType.DMA((2, 2, SLOTS)),
        ],
    )
    kernel = lambda *args: attention_kernel(*args, heads_local=heads_local, scale=scale, pieces=pieces)
    out = pl.pallas_call(
        kernel,
        grid_spec=grid_spec,
        out_shape=jax.ShapeDtypeStruct((shard_tok, width), jnp.bfloat16),
        compiler_params=pltpu.CompilerParams(dimension_semantics=("arbitrary",)),
    )(
        slot_window.reshape(-1),
        block_counts.astype(jnp.int32),
        bias,
        q_heads,
        *k_window,
        *v_window,
    )
    return lax.all_to_all(out, "head", split_axis=0, concat_axis=1, tiled=True)


def solution(mesh):
    in_specs = (
        P(("blk", "head"), None),
        P(("blk", "head"), None),
        P(("blk", "head"), None),
        P("blk", None),
        P("blk"),
        P(),
    )
    out_specs = P(("blk", "head"), None)
    return jax.shard_map(body, mesh=mesh, in_specs=in_specs, out_specs=out_specs, check_vma=False)
```

```python
import jax
import jax.numpy as jnp
from jax import lax
from jax.experimental import pallas as pl
from jax.experimental.pallas import tpu as pltpu
from jax.sharding import PartitionSpec as P

H = 48
DH = 128
TILE = 128
REACH = 3
SLOTS = 8
TILE_COUNT = 8

PIECE_OF_OFFSET = ((4, 1, 5, 0, 3, 2, 6), (5, 1, 3, 0, 6, 2, 4))


def permute(block, axis, route):
    return lax.ppermute(block, axis, route)


def shift_pairs(n, distance):
    return [(i, (i + distance) % n) for i in range(n)]


def attention_kernel(sw_ref, cnt_ref, bias_ref, q_ref, *refs, heads_local, scale, pieces):
    k_hbm = refs[:pieces]
    v_hbm = refs[pieces:2 * pieces]
    o_ref, k_buf, v_buf, sem = refs[2 * pieces:]
    i = pl.program_id(0)
    steps = pl.num_programs(0)
    parity = i % 2

    def copies(step, slot, c, p, j):
        k_copy = pltpu.make_async_copy(k_hbm[p].at[:, pl.ds(j * TILE, TILE)], k_buf.at[slot, c], sem.at[0, slot, c])
        v_copy = pltpu.make_async_copy(v_hbm[p].at[pl.ds(j * TILE, TILE), :], v_buf.at[slot, c], sem.at[1, slot, c])
        return k_copy, v_copy

    def start(step, slot):
        for c in range(SLOTS):
            code = sw_ref[step * SLOTS + c]
            p_code = code // TILE_COUNT
            j = code % TILE_COUNT
            for p in range(pieces):
                @pl.when(p_code == p)
                def _():
                    for copy in copies(step, slot, c, p, j):
                        copy.start()

    @pl.when(i == 0)
    def _():
        start(0, 0)

    @pl.when(i + 1 < steps)
    def _():
        start(i + 1, 1 - parity)

    for c in range(SLOTS):
        for copy in copies(i, parity, c, 0, 0):
            copy.wait()

    count = cnt_ref[i]
    for h in range(heads_local):
        cols = slice(h * DH, (h + 1) * DH)
        q = q_ref[:, cols]
        scores = []
        for c in range(SLOTS):
            s = jnp.dot(q, k_buf[parity, c, cols, :], preferred_element_type=jnp.float32)
            s = s * scale
            s = s - bias_ref[(i * SLOTS + c) * heads_local + h]
            s = jnp.where(c < count, s, -1e30)
            scores.append(s)
        top = scores[0].max(axis=1, keepdims=True)
        for c in range(1, SLOTS):
            top = jnp.maximum(top, scores[c].max(axis=1, keepdims=True))
        total = jnp.zeros((TILE, 1), jnp.float32)
        acc = jnp.zeros((TILE, DH), jnp.float32)
        for c in range(SLOTS):
            w = jnp.exp(scores[c] - top).astype(jnp.bfloat16)
            total = total + w.astype(jnp.float32).sum(axis=1, keepdims=True)
            acc = acc + jnp.dot(w, v_buf[parity, c, :, cols], preferred_element_type=jnp.float32)
        o_ref[:, cols] = (acc / total).astype(o_ref.dtype)


def exchange(local, axis, n):
    swap = [(i, i ^ 1) for i in range(n)]
    from_left2 = permute(local, "blk", shift_pairs(n, 2))
    from_right2 = permute(local, "blk", shift_pairs(n, -2))
    other_core = permute(local, "blk", swap)
    core = lax.axis_index("blk") % 2
    forward = jnp.where(core == 1, from_left2, from_right2)
    cross_route = [((i, (i + 1) % n) if i % 2 == 1 else (i, (i - 1) % n)) for i in range(n)]
    across = permute(forward, "blk", cross_route)
    other_left2 = permute(from_left2, "blk", swap)
    other_right2 = permute(from_right2, "blk", swap)
    return [local, from_left2, from_right2, other_core, across, other_left2, other_right2]


def body(queries, key_states, value_states, block_lists, block_counts, tile_order):
    cycle_size = lax.axis_size("blk")
    group_size = lax.axis_size("head")
    heads_local = H // group_size
    k_heads = lax.all_to_all(key_states, "head", split_axis=1, concat_axis=0, tiled=True)
    k_window = exchange(k_heads.T, 1, cycle_size)
    v_heads = lax.all_to_all(value_states, "head", split_axis=1, concat_axis=0, tiled=True)
    v_window = exchange(v_heads, 0, cycle_size)
    queries, k_window = lax.optimization_barrier((queries, k_window))
    q_heads = lax.all_to_all(queries, "head", split_axis=1, concat_axis=0, tiled=True)
    shard_tok = q_heads.shape[0]
    tile_count = shard_tok // TILE
    width = heads_local * DH

    blk_index = lax.axis_index("blk")
    core = blk_index % 2
    shard_of = block_lists // tile_count
    offset = (shard_of - blk_index + REACH) % cycle_size
    table = jnp.array(PIECE_OF_OFFSET, dtype=jnp.int32)[core]
    slot_window = (table[offset] * tile_count + block_lists % tile_count).astype(jnp.int32)
    query_tile = blk_index * tile_count + jnp.arange(tile_count, dtype=jnp.int32)
    distance = (
        jnp.abs(tile_order[query_tile][:, None] - tile_order[block_lists]).astype(jnp.float32)
        / tile_order.shape[0]
    )
    head_index = lax.axis_index("head") * heads_local + jnp.arange(heads_local, dtype=jnp.int32)
    slopes = 8.0 * jnp.power(2.0, -8.0 * head_index.astype(jnp.float32) / H)
    bias = (slopes[None, None, :] * distance[:, :, None]).reshape(-1)
    scale = DH ** (-0.5)

    assert tile_count == TILE_COUNT
    pieces = len(k_window)
    any_spec = pl.BlockSpec(memory_space=pl.ANY)
    in_specs = (
        [pl.BlockSpec(memory_space=pltpu.SMEM), pl.BlockSpec((TILE, width), lambda i, sw, cnt: (i, 0))]
        + [any_spec] * (2 * pieces)
    )
    grid_spec = pltpu.PrefetchScalarGridSpec(
        num_scalar_prefetch=2,
        grid=(tile_count,),
        in_specs=in_specs,
        out_specs=pl.BlockSpec((TILE, width), lambda i, sw, cnt: (i, 0)),
        scratch_shapes=[
            pltpu.VMEM((2, SLOTS, width, TILE), jnp.bfloat16),
            pltpu.VMEM((2, SLOTS, TILE, width), jnp.bfloat16),
            pltpu.SemaphoreType.DMA((2, 2, SLOTS)),
        ],
    )
    kernel = lambda *args: attention_kernel(*args, heads_local=heads_local, scale=scale, pieces=pieces)
    out = pl.pallas_call(
        kernel,
        grid_spec=grid_spec,
        out_shape=jax.ShapeDtypeStruct((shard_tok, width), jnp.bfloat16),
        compiler_params=pltpu.CompilerParams(dimension_semantics=("arbitrary",)),
    )(
        slot_window.reshape(-1),
        block_counts.astype(jnp.int32),
        bias,
        q_heads,
        *k_window,
        *v_window,
    )
    return lax.all_to_all(out, "head", split_axis=0, concat_axis=1, tiled=True)


def solution(mesh):
    in_specs = (
        P(("blk", "head"), None),
        P(("blk", "head"), None),
        P(("blk", "head"), None),
        P("blk", None),
        P("blk"),
        P(),
    )
    out_specs = P(("blk", "head"), None)
    return jax.shard_map(body, mesh=mesh, in_specs=in_specs, out_specs=out_specs, check_vma=False)
```

```python
import jax
import jax.numpy as jnp
from jax import lax
from jax.experimental import pallas as pl
from jax.experimental.pallas import tpu as pltpu
from jax.sharding import PartitionSpec as P

H = 48
DH = 128
TILE = 128
REACH = 3
SLOTS = 8
TILE_COUNT = 8

PIECE_OF_OFFSET = ((4, 1, 5, 0, 3, 2, 6), (5, 1, 3, 0, 6, 2, 4))


def permute(block, axis, route):
    return lax.ppermute(block, axis, route)


def shift_pairs(n, distance):
    return [(i, (i + distance) % n) for i in range(n)]


def attention_kernel(sw_ref, cnt_ref, bias_ref, q_ref, *refs, heads_local, scale, pieces):
    k_hbm = refs[:pieces]
    v_hbm = refs[pieces:2 * pieces]
    o_ref, k_buf, v_buf, sem = refs[2 * pieces:]
    i = pl.program_id(0)
    steps = pl.num_programs(0)
    parity = i % 2

    def copies(step, slot, c, p, j):
        k_copy = pltpu.make_async_copy(k_hbm[p].at[:, pl.ds(j * TILE, TILE)], k_buf.at[slot, c], sem.at[0, slot, c])
        v_copy = pltpu.make_async_copy(v_hbm[p].at[pl.ds(j * TILE, TILE), :], v_buf.at[slot, c], sem.at[1, slot, c])
        return k_copy, v_copy

    def start(step, slot):
        for c in range(SLOTS):
            code = sw_ref[step * SLOTS + c]
            p_code = code // TILE_COUNT
            j = code % TILE_COUNT
            for p in range(pieces):
                @pl.when(p_code == p)
                def _():
                    for copy in copies(step, slot, c, p, j):
                        copy.start()

    @pl.when(i == 0)
    def _():
        start(0, 0)

    @pl.when(i + 1 < steps)
    def _():
        start(i + 1, 1 - parity)

    for c in range(SLOTS):
        for copy in copies(i, parity, c, 0, 0):
            copy.wait()

    count = cnt_ref[i]
    for h in range(heads_local):
        cols = slice(h * DH, (h + 1) * DH)
        q = q_ref[:, cols]
        scores = []
        for c in range(SLOTS):
            s = jnp.dot(q, k_buf[parity, c, cols, :], preferred_element_type=jnp.float32)
            s = s * scale
            s = s - bias_ref[(i * SLOTS + c) * heads_local + h]
            s = jnp.where(c < count, s, -1e30)
            scores.append(s)
        top = scores[0].max(axis=1, keepdims=True)
        for c in range(1, SLOTS):
            top = jnp.maximum(top, scores[c].max(axis=1, keepdims=True))
        total = jnp.zeros((TILE, 1), jnp.float32)
        acc = jnp.zeros((TILE, DH), jnp.float32)
        for c in range(SLOTS):
            w = jnp.exp(scores[c] - top).astype(jnp.bfloat16)
            total = total + w.astype(jnp.float32).sum(axis=1, keepdims=True)
            acc = acc + jnp.dot(w, v_buf[parity, c, :, cols], preferred_element_type=jnp.float32)
        o_ref[:, cols] = (acc / total).astype(o_ref.dtype)


def exchange(local, axis, n):
    swap = [(i, i ^ 1) for i in range(n)]
    from_left2 = permute(local, "blk", shift_pairs(n, 2))
    from_right2 = permute(local, "blk", shift_pairs(n, -2))
    other_core = permute(local, "blk", swap)
    core = lax.axis_index("blk") % 2
    forward = jnp.where(core == 1, from_left2, from_right2)
    cross_route = [((i, (i + 1) % n) if i % 2 == 1 else (i, (i - 1) % n)) for i in range(n)]
    across = permute(forward, "blk", cross_route)
    other_left2 = permute(from_left2, "blk", swap)
    other_right2 = permute(from_right2, "blk", swap)
    return [local, from_left2, from_right2, other_core, across, other_left2, other_right2]


def body(queries, key_states, value_states, block_lists, block_counts, tile_order):
    cycle_size = lax.axis_size("blk")
    group_size = lax.axis_size("head")
    heads_local = H // group_size
    k_heads = lax.all_to_all(key_states, "head", split_axis=1, concat_axis=0, tiled=True)
    k_window = exchange(k_heads.T, 1, cycle_size)
    v_and_q = jnp.stack((value_states, queries))
    v_heads, q_heads = lax.all_to_all(v_and_q, "head", split_axis=2, concat_axis=1, tiled=True)
    v_window = exchange(v_heads, 0, cycle_size)
    shard_tok = q_heads.shape[0]
    tile_count = shard_tok // TILE
    width = heads_local * DH

    blk_index = lax.axis_index("blk")
    core = blk_index % 2
    shard_of = block_lists // tile_count
    offset = (shard_of - blk_index + REACH) % cycle_size
    table = jnp.array(PIECE_OF_OFFSET, dtype=jnp.int32)[core]
    slot_window = (table[offset] * tile_count + block_lists % tile_count).astype(jnp.int32)
    query_tile = blk_index * tile_count + jnp.arange(tile_count, dtype=jnp.int32)
    distance = (
        jnp.abs(tile_order[query_tile][:, None] - tile_order[block_lists]).astype(jnp.float32)
        / tile_order.shape[0]
    )
    head_index = lax.axis_index("head") * heads_local + jnp.arange(heads_local, dtype=jnp.int32)
    slopes = 8.0 * jnp.power(2.0, -8.0 * head_index.astype(jnp.float32) / H)
    bias = (slopes[None, None, :] * distance[:, :, None]).reshape(-1)
    scale = DH ** (-0.5)

    assert tile_count == TILE_COUNT
    pieces = len(k_window)
    any_spec = pl.BlockSpec(memory_space=pl.ANY)
    in_specs = (
        [pl.BlockSpec(memory_space=pltpu.SMEM), pl.BlockSpec((TILE, width), lambda i, sw, cnt: (i, 0))]
        + [any_spec] * (2 * pieces)
    )
    grid_spec = pltpu.PrefetchScalarGridSpec(
        num_scalar_prefetch=2,
        grid=(tile_count,),
        in_specs=in_specs,
        out_specs=pl.BlockSpec((TILE, width), lambda i, sw, cnt: (i, 0)),
        scratch_shapes=[
            pltpu.VMEM((2, SLOTS, width, TILE), jnp.bfloat16),
            pltpu.VMEM((2, SLOTS, TILE, width), jnp.bfloat16),
            pltpu.SemaphoreType.DMA((2, 2, SLOTS)),
        ],
    )
    kernel = lambda *args: attention_kernel(*args, heads_local=heads_local, scale=scale, pieces=pieces)
    out = pl.pallas_call(
        kernel,
        grid_spec=grid_spec,
        out_shape=jax.ShapeDtypeStruct((shard_tok, width), jnp.bfloat16),
        compiler_params=pltpu.CompilerParams(dimension_semantics=("arbitrary",)),
    )(
        slot_window.reshape(-1),
        block_counts.astype(jnp.int32),
        bias,
        q_heads,
        *k_window,
        *v_window,
    )
    return lax.all_to_all(out, "head", split_axis=0, concat_axis=1, tiled=True)


def solution(mesh):
    in_specs = (
        P(("blk", "head"), None),
        P(("blk", "head"), None),
        P(("blk", "head"), None),
        P("blk", None),
        P("blk"),
        P(),
    )
    out_specs = P(("blk", "head"), None)
    return jax.shard_map(body, mesh=mesh, in_specs=in_specs, out_specs=out_specs, check_vma=False)
```

```python
import jax
import jax.numpy as jnp
from jax import lax
from jax.experimental import pallas as pl
from jax.experimental.pallas import tpu as pltpu
from jax.sharding import PartitionSpec as P

H = 48
DH = 128
TILE = 128
REACH = 3
SLOTS = 8
TILE_COUNT = 8

PIECE_OF_OFFSET = ((4, 1, 6, 0, 3, 2, 7), (6, 1, 3, 0, 7, 2, 5))


def permute(block, axis, route):
    return lax.ppermute(block, axis, route)


def shift_pairs(n, distance):
    return [(i, (i + distance) % n) for i in range(n)]


def attention_kernel(sw_ref, cnt_ref, bias_ref, q_ref, *refs, heads_local, scale, pieces):
    k_hbm = refs[:pieces]
    v_hbm = refs[pieces:2 * pieces]
    o_ref, k_buf, v_buf, sem = refs[2 * pieces:]
    i = pl.program_id(0)
    steps = pl.num_programs(0)
    parity = i % 2

    def copies(step, slot, c, p, j):
        k_copy = pltpu.make_async_copy(k_hbm[p].at[:, pl.ds(j * TILE, TILE)], k_buf.at[slot, c], sem.at[0, slot, c])
        v_copy = pltpu.make_async_copy(v_hbm[p].at[pl.ds(j * TILE, TILE), :], v_buf.at[slot, c], sem.at[1, slot, c])
        return k_copy, v_copy

    def start(step, slot):
        for c in range(SLOTS):
            code = sw_ref[step * SLOTS + c]
            p_code = code // TILE_COUNT
            j = code % TILE_COUNT
            for p in range(pieces):
                @pl.when(p_code == p)
                def _():
                    for copy in copies(step, slot, c, p, j):
                        copy.start()

    @pl.when(i == 0)
    def _():
        start(0, 0)

    @pl.when(i + 1 < steps)
    def _():
        start(i + 1, 1 - parity)

    for c in range(SLOTS):
        for copy in copies(i, parity, c, 0, 0):
            copy.wait()

    count = cnt_ref[i]
    for h in range(heads_local):
        cols = slice(h * DH, (h + 1) * DH)
        q = q_ref[:, cols]
        scores = []
        for c in range(SLOTS):
            s = jnp.dot(q, k_buf[parity, c, cols, :], preferred_element_type=jnp.float32)
            s = s * scale
            s = s - bias_ref[(i * SLOTS + c) * heads_local + h]
            s = jnp.where(c < count, s, -1e30)
            scores.append(s)
        top = scores[0].max(axis=1, keepdims=True)
        for c in range(1, SLOTS):
            top = jnp.maximum(top, scores[c].max(axis=1, keepdims=True))
        total = jnp.zeros((TILE, 1), jnp.float32)
        acc = jnp.zeros((TILE, DH), jnp.float32)
        for c in range(SLOTS):
            w = jnp.exp(scores[c] - top).astype(jnp.bfloat16)
            total = total + w.astype(jnp.float32).sum(axis=1, keepdims=True)
            acc = acc + jnp.dot(w, v_buf[parity, c, :, cols], preferred_element_type=jnp.float32)
        o_ref[:, cols] = (acc / total).astype(o_ref.dtype)


def exchange(local, axis, n):
    swap = [(i, i ^ 1) for i in range(n)]
    from_left2 = permute(local, "blk", shift_pairs(n, 2))
    from_right2 = permute(local, "blk", shift_pairs(n, -2))
    other_core = permute(local, "blk", swap)
    odd_ahead = permute(from_left2, "blk", [(i, (i + 1) % n) for i in range(1, n, 2)])
    even_back = permute(from_right2, "blk", [(i, (i - 1) % n) for i in range(0, n, 2)])
    other_left2 = permute(from_left2, "blk", swap)
    other_right2 = permute(from_right2, "blk", swap)
    return [local, from_left2, from_right2, other_core, odd_ahead, even_back, other_left2, other_right2]


def body(queries, key_states, value_states, block_lists, block_counts, tile_order):
    cycle_size = lax.axis_size("blk")
    group_size = lax.axis_size("head")
    heads_local = H // group_size
    k_heads = lax.all_to_all(key_states, "head", split_axis=1, concat_axis=0, tiled=True)
    k_window = exchange(k_heads.T, 1, cycle_size)
    v_and_q = jnp.stack((value_states, queries))
    v_heads, q_heads = lax.all_to_all(v_and_q, "head", split_axis=2, concat_axis=1, tiled=True)
    v_window = exchange(v_heads, 0, cycle_size)
    shard_tok = q_heads.shape[0]
    tile_count = shard_tok // TILE
    width = heads_local * DH

    blk_index = lax.axis_index("blk")
    core = blk_index % 2
    shard_of = block_lists // tile_count
    offset = (shard_of - blk_index + REACH) % cycle_size
    table = jnp.array(PIECE_OF_OFFSET, dtype=jnp.int32)[core]
    slot_window = (table[offset] * tile_count + block_lists % tile_count).astype(jnp.int32)
    query_tile = blk_index * tile_count + jnp.arange(tile_count, dtype=jnp.int32)
    distance = (
        jnp.abs(tile_order[query_tile][:, None] - tile_order[block_lists]).astype(jnp.float32)
        / tile_order.shape[0]
    )
    head_index = lax.axis_index("head") * heads_local + jnp.arange(heads_local, dtype=jnp.int32)
    slopes = 8.0 * jnp.power(2.0, -8.0 * head_index.astype(jnp.float32) / H)
    bias = (slopes[None, None, :] * distance[:, :, None]).reshape(-1)
    scale = DH ** (-0.5)

    assert tile_count == TILE_COUNT
    pieces = len(k_window)
    any_spec = pl.BlockSpec(memory_space=pl.ANY)
    in_specs = (
        [pl.BlockSpec(memory_space=pltpu.SMEM), pl.BlockSpec((TILE, width), lambda i, sw, cnt: (i, 0))]
        + [any_spec] * (2 * pieces)
    )
    grid_spec = pltpu.PrefetchScalarGridSpec(
        num_scalar_prefetch=2,
        grid=(tile_count,),
        in_specs=in_specs,
        out_specs=pl.BlockSpec((TILE, width), lambda i, sw, cnt: (i, 0)),
        scratch_shapes=[
            pltpu.VMEM((2, SLOTS, width, TILE), jnp.bfloat16),
            pltpu.VMEM((2, SLOTS, TILE, width), jnp.bfloat16),
            pltpu.SemaphoreType.DMA((2, 2, SLOTS)),
        ],
    )
    kernel = lambda *args: attention_kernel(*args, heads_local=heads_local, scale=scale, pieces=pieces)
    out = pl.pallas_call(
        kernel,
        grid_spec=grid_spec,
        out_shape=jax.ShapeDtypeStruct((shard_tok, width), jnp.bfloat16),
        compiler_params=pltpu.CompilerParams(dimension_semantics=("arbitrary",)),
    )(
        slot_window.reshape(-1),
        block_counts.astype(jnp.int32),
        bias,
        q_heads,
        *k_window,
        *v_window,
    )
    return lax.all_to_all(out, "head", split_axis=0, concat_axis=1, tiled=True)


def solution(mesh):
    in_specs = (
        P(("blk", "head"), None),
        P(("blk", "head"), None),
        P(("blk", "head"), None),
        P("blk", None),
        P("blk"),
        P(),
    )
    out_specs = P(("blk", "head"), None)
    return jax.shard_map(body, mesh=mesh, in_specs=in_specs, out_specs=out_specs, check_vma=False)
```

```python
import jax
import jax.numpy as jnp
from jax import lax
from jax.experimental import pallas as pl
from jax.experimental.pallas import tpu as pltpu
from jax.sharding import PartitionSpec as P

H = 48
DH = 128
TILE = 128
REACH = 3
SLOTS = 8
TILE_COUNT = 8

PIECE_OF_OFFSET = ((4, 1, 5, 0, 3, 2, 6), (5, 1, 3, 0, 6, 2, 4))


def permute(block, axis, route):
    return lax.ppermute(block, axis, route)


def shift_pairs(n, distance):
    return [(i, (i + distance) % n) for i in range(n)]


def attention_kernel(sw_ref, cnt_ref, bias_ref, q_ref, *refs, heads_local, scale, pieces):
    k_hbm = refs[:pieces]
    v_hbm = refs[pieces:2 * pieces]
    o_ref, k_buf, v_buf, sem = refs[2 * pieces:]
    i = pl.program_id(0)
    steps = pl.num_programs(0)
    parity = i % 2

    def copies(step, slot, c, p, j):
        k_copy = pltpu.make_async_copy(k_hbm[p].at[:, pl.ds(j * TILE, TILE)], k_buf.at[slot, c], sem.at[0, slot, c])
        v_copy = pltpu.make_async_copy(v_hbm[p].at[pl.ds(j * TILE, TILE), :], v_buf.at[slot, c], sem.at[1, slot, c])
        return k_copy, v_copy

    def start(step, slot):
        for c in range(SLOTS):
            code = sw_ref[step * SLOTS + c]
            p_code = code // TILE_COUNT
            j = code % TILE_COUNT
            for p in range(pieces):
                @pl.when(p_code == p)
                def _():
                    for copy in copies(step, slot, c, p, j):
                        copy.start()

    @pl.when(i == 0)
    def _():
        start(0, 0)

    @pl.when(i + 1 < steps)
    def _():
        start(i + 1, 1 - parity)

    for c in range(SLOTS):
        for copy in copies(i, parity, c, 0, 0):
            copy.wait()

    count = cnt_ref[i]
    for h in range(heads_local):
        cols = slice(h * DH, (h + 1) * DH)
        q = q_ref[:, cols]
        scores = []
        for c in range(SLOTS):
            s = jnp.dot(q, k_buf[parity, c, cols, :], preferred_element_type=jnp.float32)
            s = s * scale
            s = s - bias_ref[(i * SLOTS + c) * heads_local + h]
            s = jnp.where(c < count, s, -1e30)
            scores.append(s)
        top = scores[0].max(axis=1, keepdims=True)
        for c in range(1, SLOTS):
            top = jnp.maximum(top, scores[c].max(axis=1, keepdims=True))
        total = jnp.zeros((TILE, 1), jnp.float32)
        acc = jnp.zeros((TILE, DH), jnp.float32)
        for c in range(SLOTS):
            w = jnp.exp(scores[c] - top).astype(jnp.bfloat16)
            total = total + w.astype(jnp.float32).sum(axis=1, keepdims=True)
            acc = acc + jnp.dot(w, v_buf[parity, c, :, cols], preferred_element_type=jnp.float32)
        o_ref[:, cols] = (acc / total).astype(o_ref.dtype)


def exchange(local, axis, n):
    swap = [(i, i ^ 1) for i in range(n)]
    from_left2 = permute(local, "blk", shift_pairs(n, 2))
    from_right2 = permute(local, "blk", shift_pairs(n, -2))
    other_core = permute(local, "blk", swap)
    core = lax.axis_index("blk") % 2
    forward = jnp.where(core == 1, from_left2, from_right2)
    cross_route = [((i, (i + 1) % n) if i % 2 == 1 else (i, (i - 1) % n)) for i in range(n)]
    across = permute(forward, "blk", cross_route)
    other_left2 = permute(from_left2, "blk", swap)
    other_right2 = permute(from_right2, "blk", swap)
    return [local, from_left2, from_right2, other_core, across, other_left2, other_right2]


def body(queries, key_states, value_states, block_lists, block_counts, tile_order):
    cycle_size = lax.axis_size("blk")
    group_size = lax.axis_size("head")
    heads_local = H // group_size
    k_heads = lax.all_to_all(key_states, "head", split_axis=1, concat_axis=0, tiled=True)
    k_heads, value_states, queries = lax.optimization_barrier((k_heads, value_states, queries))
    v_and_q = jnp.stack((value_states, queries))
    k_window = exchange(k_heads.T, 1, cycle_size)
    v_heads, q_heads = lax.all_to_all(v_and_q, "head", split_axis=2, concat_axis=1, tiled=True)
    v_window = exchange(v_heads, 0, cycle_size)
    shard_tok = q_heads.shape[0]
    tile_count = shard_tok // TILE
    width = heads_local * DH

    blk_index = lax.axis_index("blk")
    core = blk_index % 2
    shard_of = block_lists // tile_count
    offset = (shard_of - blk_index + REACH) % cycle_size
    table = jnp.array(PIECE_OF_OFFSET, dtype=jnp.int32)[core]
    slot_window = (table[offset] * tile_count + block_lists % tile_count).astype(jnp.int32)
    query_tile = blk_index * tile_count + jnp.arange(tile_count, dtype=jnp.int32)
    distance = (
        jnp.abs(tile_order[query_tile][:, None] - tile_order[block_lists]).astype(jnp.float32)
        / tile_order.shape[0]
    )
    head_index = lax.axis_index("head") * heads_local + jnp.arange(heads_local, dtype=jnp.int32)
    slopes = 8.0 * jnp.power(2.0, -8.0 * head_index.astype(jnp.float32) / H)
    bias = (slopes[None, None, :] * distance[:, :, None]).reshape(-1)
    scale = DH ** (-0.5)

    assert tile_count == TILE_COUNT
    pieces = len(k_window)
    any_spec = pl.BlockSpec(memory_space=pl.ANY)
    in_specs = (
        [pl.BlockSpec(memory_space=pltpu.SMEM), pl.BlockSpec((TILE, width), lambda i, sw, cnt: (i, 0))]
        + [any_spec] * (2 * pieces)
    )
    grid_spec = pltpu.PrefetchScalarGridSpec(
        num_scalar_prefetch=2,
        grid=(tile_count,),
        in_specs=in_specs,
        out_specs=pl.BlockSpec((TILE, width), lambda i, sw, cnt: (i, 0)),
        scratch_shapes=[
            pltpu.VMEM((2, SLOTS, width, TILE), jnp.bfloat16),
            pltpu.VMEM((2, SLOTS, TILE, width), jnp.bfloat16),
            pltpu.SemaphoreType.DMA((2, 2, SLOTS)),
        ],
    )
    kernel = lambda *args: attention_kernel(*args, heads_local=heads_local, scale=scale, pieces=pieces)
    out = pl.pallas_call(
        kernel,
        grid_spec=grid_spec,
        out_shape=jax.ShapeDtypeStruct((shard_tok, width), jnp.bfloat16),
        compiler_params=pltpu.CompilerParams(dimension_semantics=("arbitrary",)),
    )(
        slot_window.reshape(-1),
        block_counts.astype(jnp.int32),
        bias,
        q_heads,
        *k_window,
        *v_window,
    )
    return lax.all_to_all(out, "head", split_axis=0, concat_axis=1, tiled=True)


def solution(mesh):
    in_specs = (
        P(("blk", "head"), None),
        P(("blk", "head"), None),
        P(("blk", "head"), None),
        P("blk", None),
        P("blk"),
        P(),
    )
    out_specs = P(("blk", "head"), None)
    return jax.shard_map(body, mesh=mesh, in_specs=in_specs, out_specs=out_specs, check_vma=False)
```

```python
import jax
import jax.numpy as jnp
from jax import lax
from jax.experimental import pallas as pl
from jax.experimental.pallas import tpu as pltpu
from jax.sharding import PartitionSpec as P

H = 48
DH = 128
TILE = 128
REACH = 3
SLOTS = 8
TILE_COUNT = 8

PIECE_OF_OFFSET = ((4, 1, 5, 0, 3, 2, 6), (5, 1, 3, 0, 6, 2, 4))


def permute(block, axis, route):
    return lax.ppermute(block, axis, route)


def shift_pairs(n, distance):
    return [(i, (i + distance) % n) for i in range(n)]


def attention_kernel(sw_ref, cnt_ref, bias_ref, q_ref, *refs, heads_local, scale, pieces):
    k_hbm = refs[:pieces]
    v_hbm = refs[pieces:2 * pieces]
    o_ref, k_buf, v_buf, sem = refs[2 * pieces:]
    i = pl.program_id(0)
    steps = pl.num_programs(0)
    parity = i % 2

    def copies(step, slot, c, p, j):
        k_copy = pltpu.make_async_copy(k_hbm[p].at[:, pl.ds(j * TILE, TILE)], k_buf.at[slot, c], sem.at[0, slot, c])
        v_copy = pltpu.make_async_copy(v_hbm[p].at[pl.ds(j * TILE, TILE), :], v_buf.at[slot, c], sem.at[1, slot, c])
        return k_copy, v_copy

    def start(step, slot):
        for c in range(SLOTS):
            code = sw_ref[step * SLOTS + c]
            p_code = code // TILE_COUNT
            j = code % TILE_COUNT
            for p in range(pieces):
                @pl.when(p_code == p)
                def _():
                    for copy in copies(step, slot, c, p, j):
                        copy.start()

    @pl.when(i == 0)
    def _():
        start(0, 0)

    @pl.when(i + 1 < steps)
    def _():
        start(i + 1, 1 - parity)

    for c in range(SLOTS):
        for copy in copies(i, parity, c, 0, 0):
            copy.wait()

    count = cnt_ref[i]
    for h in range(heads_local):
        cols = slice(h * DH, (h + 1) * DH)
        q = q_ref[:, cols]
        scores = []
        for c in range(SLOTS):
            s = jnp.dot(q, k_buf[parity, c, cols, :], preferred_element_type=jnp.float32)
            s = s * scale
            s = s - bias_ref[(i * SLOTS + c) * heads_local + h]
            s = jnp.where(c < count, s, -1e30)
            scores.append(s)
        top = scores[0].max(axis=1, keepdims=True)
        for c in range(1, SLOTS):
            top = jnp.maximum(top, scores[c].max(axis=1, keepdims=True))
        total = jnp.zeros((TILE, 1), jnp.float32)
        acc = jnp.zeros((TILE, DH), jnp.float32)
        for c in range(SLOTS):
            w = jnp.exp(scores[c] - top).astype(jnp.bfloat16)
            total = total + w.astype(jnp.float32).sum(axis=1, keepdims=True)
            acc = acc + jnp.dot(w, v_buf[parity, c, :, cols], preferred_element_type=jnp.float32)
        o_ref[:, cols] = (acc / total).astype(o_ref.dtype)


def exchange(local, axis, n):
    swap = [(i, i ^ 1) for i in range(n)]
    from_left2 = permute(local, "blk", shift_pairs(n, 2))
    from_right2 = permute(local, "blk", shift_pairs(n, -2))
    other_core = permute(local, "blk", swap)
    core = lax.axis_index("blk") % 2
    forward = jnp.where(core == 1, from_left2, from_right2)
    cross_route = [((i, (i + 1) % n) if i % 2 == 1 else (i, (i - 1) % n)) for i in range(n)]
    across = permute(forward, "blk", cross_route)
    other_left2 = permute(from_left2, "blk", swap)
    other_right2 = permute(from_right2, "blk", swap)
    return [local, from_left2, from_right2, other_core, across, other_left2, other_right2]


def body(queries, key_states, value_states, block_lists, block_counts, tile_order):
    cycle_size = lax.axis_size("blk")
    group_size = lax.axis_size("head")
    heads_local = H // group_size
    v_heads = lax.all_to_all(value_states, "head", split_axis=1, concat_axis=0, tiled=True)
    v_window = exchange(v_heads, 0, cycle_size)
    k_and_q = jnp.stack((key_states, queries))
    k_heads, q_heads = lax.all_to_all(k_and_q, "head", split_axis=2, concat_axis=1, tiled=True)
    k_window = exchange(k_heads.T, 1, cycle_size)
    shard_tok = q_heads.shape[0]
    tile_count = shard_tok // TILE
    width = heads_local * DH

    blk_index = lax.axis_index("blk")
    core = blk_index % 2
    shard_of = block_lists // tile_count
    offset = (shard_of - blk_index + REACH) % cycle_size
    table = jnp.array(PIECE_OF_OFFSET, dtype=jnp.int32)[core]
    slot_window = (table[offset] * tile_count + block_lists % tile_count).astype(jnp.int32)
    query_tile = blk_index * tile_count + jnp.arange(tile_count, dtype=jnp.int32)
    distance = (
        jnp.abs(tile_order[query_tile][:, None] - tile_order[block_lists]).astype(jnp.float32)
        / tile_order.shape[0]
    )
    head_index = lax.axis_index("head") * heads_local + jnp.arange(heads_local, dtype=jnp.int32)
    slopes = 8.0 * jnp.power(2.0, -8.0 * head_index.astype(jnp.float32) / H)
    bias = (slopes[None, None, :] * distance[:, :, None]).reshape(-1)
    scale = DH ** (-0.5)

    assert tile_count == TILE_COUNT
    pieces = len(k_window)
    any_spec = pl.BlockSpec(memory_space=pl.ANY)
    in_specs = (
        [pl.BlockSpec(memory_space=pltpu.SMEM), pl.BlockSpec((TILE, width), lambda i, sw, cnt: (i, 0))]
        + [any_spec] * (2 * pieces)
    )
    grid_spec = pltpu.PrefetchScalarGridSpec(
        num_scalar_prefetch=2,
        grid=(tile_count,),
        in_specs=in_specs,
        out_specs=pl.BlockSpec((TILE, width), lambda i, sw, cnt: (i, 0)),
        scratch_shapes=[
            pltpu.VMEM((2, SLOTS, width, TILE), jnp.bfloat16),
            pltpu.VMEM((2, SLOTS, TILE, width), jnp.bfloat16),
            pltpu.SemaphoreType.DMA((2, 2, SLOTS)),
        ],
    )
    kernel = lambda *args: attention_kernel(*args, heads_local=heads_local, scale=scale, pieces=pieces)
    out = pl.pallas_call(
        kernel,
        grid_spec=grid_spec,
        out_shape=jax.ShapeDtypeStruct((shard_tok, width), jnp.bfloat16),
        compiler_params=pltpu.CompilerParams(dimension_semantics=("arbitrary",)),
    )(
        slot_window.reshape(-1),
        block_counts.astype(jnp.int32),
        bias,
        q_heads,
        *k_window,
        *v_window,
    )
    return lax.all_to_all(out, "head", split_axis=0, concat_axis=1, tiled=True)


def solution(mesh):
    in_specs = (
        P(("blk", "head"), None),
        P(("blk", "head"), None),
        P(("blk", "head"), None),
        P("blk", None),
        P("blk"),
        P(),
    )
    out_specs = P(("blk", "head"), None)
    return jax.shard_map(body, mesh=mesh, in_specs=in_specs, out_specs=out_specs, check_vma=False)
```
